512 devices in a mesh: dp: 8 (over z), expert: 16 (over y, core), etp: 4 (over x).
Axes of the slice: x: 4, y: 8, z: 8, core: 2. Of those that a mesh axis runs over, the one named last changes fastest.
Arguments:
- tokens: bfloat16 [3072, 4096], P(('dp', 'expert')), may hold values from -6 to 6
- cotangent: bfloat16 [3072, 4096], P(('dp', 'expert')), may hold values from -3 to 3
- route_weights: float32 [3072, 8], P(('dp', 'expert')), may hold values from 0.05 to 0.3
- expert_ids: int32 [3072, 8], P(('dp', 'expert')), may hold values from 0 to 15, as said below
- w_gate: bfloat16 [16, 1536, 4096], P('expert', 'etp', 'dp'), may hold values from -0.09375 to 0.09375
- w_up: bfloat16 [16, 1536, 4096], P('expert', 'etp', 'dp'), may hold values from -0.09375 to 0.09375
- w_down: bfloat16 [16, 1536, 4096], P('expert', 'etp', 'dp'), may hold values from -0.15625 to 0.15625
Outputs:
- mixed: bfloat16 [3072, 4096], P(('dp', 'expert'), 'etp')
- grad_tokens: bfloat16 [3072, 4096], P(('dp', 'expert'), 'etp')
- grad_gate: float32 [16, 1536, 4096], P('expert', 'etp', 'dp')
The draws below stay inside these ranges and needn't reach their ends.
Inputs may be any that keep to these rules, and one draw needn't show every extreme that they name: `expert_ids`: each row names 8 different experts. Within each aligned block of 24 rows no expert is named by more than 16 rows; in every run of 16 consecutive blocks starting at a multiple of 16, one expert is named by exactly 16 rows of every block.
All inputs are finite; a program needn't handle non-finite values.
Results may differ from the reference program's by a relative error of at most 0.012.
Values may be sent and summed in bfloat16 or wider, within the bound.
No kernel may reach another device: no remote copies, remote signals or barrier semaphores. Data moves between devices by JAX's collectives and lax.ppermute only.
A program may use at most 64 MiB of HBM per device.

```python
import math
import jax
import jax.numpy as jnp
from jax import lax

D = 4096
FF = 1536
TOK_DEV = 24
EXPERTS = 16
TOP = 8
CAP = 16
SHARE = 384
TOKENS = 3072
N_DP = 8
N_ETP = 4


def draw_expert_ids(key, part):
    blocks = TOKENS // TOK_DEV
    groups = blocks // EXPERTS
    key_hot, key_perm, key_order = jax.random.split(key, 3)
    favored = jnp.repeat(jax.random.randint(key_hot, (groups,), 0, EXPERTS), EXPERTS)
    orders = jax.vmap(lambda subkey: jax.random.permutation(subkey, EXPERTS))(jax.random.split(key_perm, blocks))
    column = jnp.arange(EXPERTS)[None, :]
    where_hot = jnp.sum(jnp.where(orders == favored[:, None], column, 0), axis=1)
    displaced = orders[:, TOP - 1]
    orders = jnp.where(column == where_hot[:, None], displaced[:, None], orders)
    orders = jnp.where(column == TOP - 1, favored[:, None], orders)
    starts = jax.vmap(lambda subkey: jax.random.permutation(subkey, TOK_DEV))(jax.random.split(key_order, blocks))
    picked = (starts[:, :, None] + jnp.arange(TOP)[None, None, :]) % EXPERTS
    chosen = jax.vmap(lambda table_row, offsets: table_row[offsets])(orders, picked)
    return chosen.reshape(TOKENS, TOP).astype(jnp.int32)


def block_levels(rng, shape, cuts, low, top_value):
    factor_of, own = 1.0, jax.random.fold_in(rng, 6)
    for dim, shards_of in cuts:
        steps = jnp.exp(jax.random.uniform(jax.random.fold_in(own, dim), (shards_of,), jnp.float32, low / len(cuts), top_value / len(cuts)))
        factor_of = factor_of * jnp.repeat(steps, shape[dim] // shards_of).reshape([-1 if axis == dim else 1 for axis in range(len(shape))])
    return factor_of


def normal_values(stream_key, dims, spread, limit, shards=(), held_as=jnp.bfloat16):
    drawn = spread * jax.random.normal(stream_key, dims, jnp.float32)
    if shards:
        drawn = drawn * block_levels(stream_key, dims, shards, -0.22, 0.18)
    return jnp.clip(drawn, -limit, limit).astype(held_as)


def setup_inputs(seed: int = 0) -> dict:
    seeds = jax.random.split(jax.random.key(seed), 8)
    return {
        "tokens": normal_values(seeds[0], (TOKENS, D), 1.0, 6.0, ((0, 128),)),
        "cotangent": normal_values(seeds[1], (TOKENS, D), 0.5, 3.0, ((0, 128),)),
        "route_weights": jnp.clip(jnp.exp(math.log(0.3) - 1.7917595 * jax.random.uniform(seeds[2], (TOKENS, TOP), jnp.float32) ** block_levels(seeds[2], (TOKENS, TOP), ((0, 128),), -0.2, 0.2)), 0.05, 0.3),
        "expert_ids": draw_expert_ids(jax.random.fold_in(seeds[7], 71), 0),
        "w_gate": normal_values(seeds[4], (EXPERTS, FF, D), D ** -0.5, 0.09375, ((0, 16), (1, 4), (2, 8))),
        "w_up": normal_values(seeds[5], (EXPERTS, FF, D), D ** -0.5, 0.09375, ((0, 16), (1, 4), (2, 8))),
        "w_down": normal_values(seeds[6], (EXPERTS, FF, D), FF ** -0.5, 0.15625, ((0, 16), (1, 4), (2, 8))),
    }


def slot_tables(expert_ids, route_weights):
    blocks = TOKENS // TOK_DEV
    routes = expert_ids.reshape(blocks, TOK_DEV, TOP)
    named_count = jnp.sum((routes[..., None] == jnp.arange(EXPERTS, dtype=jnp.int32)).astype(jnp.int32), axis=2)
    before = jnp.cumsum(named_count, axis=1) - named_count
    position = jnp.take_along_axis(before, routes, axis=2)
    block_base = (jnp.arange(blocks, dtype=jnp.int32) * (EXPERTS * CAP))[:, None, None]
    flat_slot = (block_base + routes * CAP + position).reshape(-1).astype(jnp.int32)
    token_of = jnp.broadcast_to(jnp.arange(TOKENS, dtype=jnp.int32).reshape(blocks, TOK_DEV, 1), routes.shape).reshape(-1)
    slot_owner = jnp.full((blocks * EXPERTS * CAP,), TOKENS, jnp.int32).at[flat_slot].set(token_of)
    slot_weight = jnp.zeros((blocks * EXPERTS * CAP,), jnp.float32).at[flat_slot].set(route_weights.reshape(-1))
    slot_owner = slot_owner.reshape(blocks, EXPERTS, CAP).transpose(1, 0, 2).reshape(EXPERTS, blocks * CAP)
    slot_weight = slot_weight.reshape(blocks, EXPERTS, CAP).transpose(1, 0, 2).reshape(EXPERTS, blocks * CAP)
    return slot_owner, slot_weight


def share_product(left, right):
    row_count = left.shape[0]
    left_split = left.astype(jnp.float32).reshape(row_count, N_ETP, SHARE)
    right_split = right.astype(jnp.float32).reshape(N_ETP, SHARE, D)
    return jnp.einsum("rjf,jfd->jrd", left_split, right_split)


def group_sum(slot_tokens, grads):
    row_count = slot_tokens.shape[0]
    token_split = slot_tokens.astype(jnp.float32).reshape(N_DP, row_count // N_DP, D)
    grad_split = grads.astype(jnp.float32).reshape(N_DP, row_count // N_DP, FF)
    terms = jnp.einsum("grd,grf->gfd", token_split, grad_split)
    return jnp.sum(lax.optimization_barrier(terms.astype(jnp.bfloat16)).astype(jnp.float32), axis=0)


def reference(tokens, cotangent, route_weights, expert_ids, w_gate, w_up, w_down):
    slot_owner, slot_weight = slot_tables(expert_ids, route_weights)
    padded_tokens = jnp.concatenate([tokens, jnp.zeros((1, D), tokens.dtype)], axis=0)
    padded_cot = jnp.concatenate([cotangent, jnp.zeros((1, D), cotangent.dtype)], axis=0)
    contract_last = (((1,), (1,)), ((), ()))

    def expert_step(totals, inputs):
        mixed_acc, input_acc = totals
        owner_row, weight_row, gate_w, up_w, down_w = inputs
        slot_tokens = padded_tokens[owner_row]
        slot_grads = (weight_row[:, None] * padded_cot[owner_row].astype(jnp.float32)).astype(jnp.bfloat16)
        gate_value = lax.dot_general(slot_tokens, gate_w, contract_last, preferred_element_type=jnp.float32)
        up_value = lax.dot_general(slot_tokens, up_w, contract_last, preferred_element_type=jnp.float32)
        sigmoid_gate = jax.nn.sigmoid(gate_value)
        active = gate_value * sigmoid_gate
        hidden = (active * up_value).astype(jnp.bfloat16)
        mixed_shares = share_product(hidden, down_w)
        mixed_slot = jnp.sum(lax.optimization_barrier(mixed_shares.astype(jnp.bfloat16)).astype(jnp.float32), axis=0)
        d_hidden = lax.dot_general(slot_grads, down_w, contract_last, preferred_element_type=jnp.float32)
        d_gate = (d_hidden * up_value * sigmoid_gate * (1.0 + gate_value * (1.0 - sigmoid_gate))).astype(jnp.bfloat16)
        d_up = (d_hidden * active).astype(jnp.bfloat16)
        input_shares = share_product(d_gate, gate_w) + share_product(d_up, up_w)
        input_slot = jnp.sum(lax.optimization_barrier(input_shares.astype(jnp.bfloat16)).astype(jnp.float32), axis=0)
        mixed_acc = mixed_acc.at[owner_row].add(weight_row[:, None] * mixed_slot)
        input_acc = input_acc.at[owner_row].add(input_slot)
        gate_grad = group_sum(slot_tokens, d_gate)
        return (mixed_acc, input_acc), gate_grad

    start_totals = (jnp.zeros((TOKENS + 1, D), jnp.float32), jnp.zeros((TOKENS + 1, D), jnp.float32))
    (mixed_acc, input_acc), grad_gate = lax.scan(expert_step, start_totals, (slot_owner, slot_weight, w_gate, w_up, w_down))
    return (mixed_acc[:TOKENS].astype(jnp.bfloat16), input_acc[:TOKENS].astype(jnp.bfloat16), grad_gate)
```

```python
import jax
import jax.numpy as jnp
from jax import lax
from jax.sharding import PartitionSpec as P


def on_device(tokens, cotangent, route_weights, expert_ids, w_gate, w_up, w_down):
    tok_count, model_width = tokens.shape
    top_count = expert_ids.shape[1]
    experts = lax.axis_size("expert")
    shares = lax.axis_size("etp")
    part = model_width // shares
    share_idx = lax.axis_index("etp")
    capacity = tok_count // experts * top_count + min(top_count, tok_count % experts)
    slot_rows = experts * capacity
    named_count = jnp.sum(
        (expert_ids[:, :, None] == jnp.arange(experts, dtype=jnp.int32)).astype(jnp.int32), axis=1
    )
    before = jnp.cumsum(named_count, axis=0) - named_count
    position = jnp.take_along_axis(before, expert_ids, axis=1)
    slot_index = (expert_ids * capacity + position).reshape(-1)

    tok_part = lax.dynamic_slice_in_dim(tokens, share_idx * part, part, axis=1)
    cot_part = lax.dynamic_slice_in_dim(cotangent, share_idx * part, part, axis=1)
    copies = jnp.broadcast_to(tok_part[:, None, :], (tok_count, top_count, part))
    scaled = (route_weights[:, :, None] * cot_part[:, None, :].astype(jnp.float32)).astype(jnp.bfloat16)
    both = jnp.concatenate([copies, scaled], axis=2).reshape(-1, 2 * part)
    empty_slots = jnp.zeros((slot_rows, 2 * part), jnp.bfloat16)
    send = empty_slots.at[slot_index].set(both).reshape(experts, capacity, 2 * part)
    recv = lax.all_to_all(send, "expert", split_axis=0, concat_axis=0, tiled=True)
    recv = recv.reshape(1, slot_rows, 2 * part)
    spread = jnp.broadcast_to(recv, (shares, slot_rows, 2 * part))
    gathered = lax.all_to_all(spread, "etp", split_axis=0, concat_axis=0, tiled=True)
    rows4 = gathered[:, :, :part]
    grads4 = gathered[:, :, part:]

    gate_full, up_full, down_full = (
        lax.all_gather(w_gate[0], "dp", axis=1, tiled=True),
        lax.all_gather(w_up[0], "dp", axis=1, tiled=True),
        lax.all_gather(w_down[0], "dp", axis=1, tiled=True),
    )
    hidden_units = gate_full.shape[0]
    gate4 = gate_full.reshape(hidden_units, shares, part)
    up4 = up_full.reshape(hidden_units, shares, part)
    down4 = down_full.reshape(hidden_units, shares, part)

    gate_value = jnp.einsum("jsc,fjc->sf", rows4, gate4, preferred_element_type=jnp.float32)
    up_value = jnp.einsum("jsc,fjc->sf", rows4, up4, preferred_element_type=jnp.float32)
    sigmoid_gate = jax.nn.sigmoid(gate_value)
    active = gate_value * sigmoid_gate
    hidden = (active * up_value).astype(jnp.bfloat16)
    mixed4 = jnp.einsum("sf,fjc->jsc", hidden, down4, preferred_element_type=jnp.float32).astype(
        jnp.bfloat16
    )
    d_hidden = jnp.einsum("jsc,fjc->sf", grads4, down4, preferred_element_type=jnp.float32)
    d_gate = (
        d_hidden * up_value * sigmoid_gate * (1.0 + gate_value * (1.0 - sigmoid_gate))
    ).astype(jnp.bfloat16)
    d_up = (d_hidden * active).astype(jnp.bfloat16)
    input4 = (
        jnp.einsum("sf,fjc->jsc", d_gate, gate4, preferred_element_type=jnp.float32)
        + jnp.einsum("sf,fjc->jsc", d_up, up4, preferred_element_type=jnp.float32)
    ).astype(jnp.bfloat16)
    gate_term = jnp.einsum(
        "sf,jsc->fjc", d_gate, rows4, preferred_element_type=jnp.float32
    ).astype(jnp.bfloat16).reshape(hidden_units, model_width)
    weight_grads = lax.psum_scatter(gate_term, "dp", scatter_dimension=1, tiled=True)
    grad_gate = weight_grads.astype(jnp.float32)[None]

    outs4 = jnp.concatenate([mixed4, input4], axis=2)
    summed = lax.all_to_all(outs4, "etp", split_axis=0, concat_axis=0, tiled=True)
    slot_out = jnp.sum(summed.astype(jnp.float32), axis=0).astype(jnp.bfloat16)
    back = lax.all_to_all(
        slot_out.reshape(experts, capacity, 2 * part), "expert", split_axis=0, concat_axis=0, tiled=True
    )
    token_out = back.reshape(slot_rows, 2 * part)[slot_index].reshape(tok_count, top_count, 2 * part)
    token_out = token_out.astype(jnp.float32)
    mixed = jnp.sum(route_weights[:, :, None] * token_out[:, :, :part], axis=1)
    grad_tokens = jnp.sum(token_out[:, :, part:], axis=1)
    return (mixed.astype(jnp.bfloat16), grad_tokens.astype(jnp.bfloat16), grad_gate)


def solution(mesh):
    in_specs = (
        P(("dp", "expert"), None),
        P(("dp", "expert"), None),
        P(("dp", "expert"), None),
        P(("dp", "expert"), None),
        P("expert", "etp", "dp"),
        P("expert", "etp", "dp"),
        P("expert", "etp", "dp"),
    )
    out_specs = (P(("dp", "expert"), "etp"), P(("dp", "expert"), "etp"), P("expert", "etp", "dp"))
    return jax.shard_map(
        on_device, mesh=mesh, in_specs=in_specs, out_specs=out_specs, check_vma=False
    )
```

```python
import jax
import jax.numpy as jnp
from jax import lax
from jax.sharding import PartitionSpec as P


def ring_gather(piece, axis, n, along=0):
    idx = lax.axis_index(axis)
    fwd = [(i, (i + 1) % n) for i in range(n)]
    bwd = [(i, (i - 1) % n) for i in range(n)]
    shape = list(piece.shape)
    shape.insert(along, n)
    out = jnp.zeros(shape, piece.dtype)
    put = lambda buf, val, at: lax.dynamic_update_index_in_dim(buf, val, at % n, along)
    out = put(out, piece, idx)
    left = right = piece
    half = n // 2
    for k in range(1, half):
        left = lax.ppermute(left, axis, fwd)
        right = lax.ppermute(right, axis, bwd)
        out = put(out, left, idx - k)
        out = put(out, right, idx + k)
    m = piece.shape[0] // 2
    first = lax.ppermute(left[:m], axis, fwd)
    second = lax.ppermute(right[m:], axis, bwd)
    return put(out, jnp.concatenate([first, second], axis=0), idx + half)


def ring_reduce_scatter(chunks, axis, n):
    idx = lax.axis_index(axis)
    fwd = [(i, (i + 1) % n) for i in range(n)]
    bwd = [(i, (i - 1) % n) for i in range(n)]
    pick = lambda at: lax.dynamic_index_in_dim(chunks, at % n, 0, keepdims=False).astype(jnp.float32)
    half = n // 2
    m = chunks.shape[1] // 2
    to_right = pick(idx + half)[:m]
    to_left = pick(idx - half)[m:]
    for k in range(2, half + 1):
        got_left = lax.ppermute(to_right.astype(chunks.dtype), axis, fwd).astype(jnp.float32)
        got_right = lax.ppermute(to_left.astype(chunks.dtype), axis, bwd).astype(jnp.float32)
        own_r = pick(idx + half - k + 1)
        own_l = pick(idx - half + k - 1)
        if k == 2:
            to_right = own_r.at[:m].add(got_left)
            to_left = own_l.at[m:].add(got_right)
        else:
            to_right = own_r + got_left
            to_left = own_l + got_right
    got_left = lax.ppermute(to_right.astype(chunks.dtype), axis, fwd).astype(jnp.float32)
    got_right = lax.ppermute(to_left.astype(chunks.dtype), axis, bwd).astype(jnp.float32)
    return pick(idx) + got_left + got_right


def on_device(tokens, cotangent, route_weights, expert_ids, w_gate, w_up, w_down):
    tok_count, model_width = tokens.shape
    top_count = expert_ids.shape[1]
    experts = lax.axis_size("expert")
    shares = lax.axis_size("etp")
    part = model_width // shares
    share_idx = lax.axis_index("etp")
    capacity = tok_count // experts * top_count + min(top_count, tok_count % experts)
    slot_rows = experts * capacity
    named_count = jnp.sum(
        (expert_ids[:, :, None] == jnp.arange(experts, dtype=jnp.int32)).astype(jnp.int32), axis=1
    )
    before = jnp.cumsum(named_count, axis=0) - named_count
    position = jnp.take_along_axis(before, expert_ids, axis=1)
    slot_index = (expert_ids * capacity + position).reshape(-1)

    tok_part = lax.dynamic_slice_in_dim(tokens, share_idx * part, part, axis=1)
    cot_part = lax.dynamic_slice_in_dim(cotangent, share_idx * part, part, axis=1)
    copies = jnp.broadcast_to(tok_part[:, None, :], (tok_count, top_count, part))
    scaled = (route_weights[:, :, None] * cot_part[:, None, :].astype(jnp.float32)).astype(jnp.bfloat16)
    both = jnp.concatenate([copies, scaled], axis=2).reshape(-1, 2 * part)
    empty_slots = jnp.zeros((slot_rows, 2 * part), jnp.bfloat16)
    send = empty_slots.at[slot_index].set(both).reshape(experts, capacity, 2 * part)
    recv = lax.all_to_all(send, "expert", split_axis=0, concat_axis=0, tiled=True)
    recv = recv.reshape(1, slot_rows, 2 * part)
    gathered = ring_gather(recv[0], "etp", shares)
    rows4 = gathered[:, :, :part]
    grads4 = gathered[:, :, part:]

    gate_full, up_full, down_full = (
        lax.all_gather(w_gate[0], "dp", axis=1, tiled=True),
        lax.all_gather(w_up[0], "dp", axis=1, tiled=True),
        ring_gather(w_down[0], "dp", lax.axis_size("dp"), along=1).reshape(w_down.shape[1], -1),
    )
    hidden_units = gate_full.shape[0]
    gate4 = gate_full.reshape(hidden_units, shares, part)
    up4 = up_full.reshape(hidden_units, shares, part)
    down4 = down_full.reshape(hidden_units, shares, part)

    gate_value = jnp.einsum("jsc,fjc->sf", rows4, gate4, preferred_element_type=jnp.float32)
    up_value = jnp.einsum("jsc,fjc->sf", rows4, up4, preferred_element_type=jnp.float32)
    sigmoid_gate = jax.nn.sigmoid(gate_value)
    active = gate_value * sigmoid_gate
    hidden = (active * up_value).astype(jnp.bfloat16)
    mixed4 = jnp.einsum("sf,fjc->jsc", hidden, down4, preferred_element_type=jnp.float32).astype(
        jnp.bfloat16
    )
    d_hidden = jnp.einsum("jsc,fjc->sf", grads4, down4, preferred_element_type=jnp.float32)
    d_gate = (
        d_hidden * up_value * sigmoid_gate * (1.0 + gate_value * (1.0 - sigmoid_gate))
    ).astype(jnp.bfloat16)
    d_up = (d_hidden * active).astype(jnp.bfloat16)
    input4 = (
        jnp.einsum("sf,fjc->jsc", d_gate, gate4, preferred_element_type=jnp.float32)
        + jnp.einsum("sf,fjc->jsc", d_up, up4, preferred_element_type=jnp.float32)
    ).astype(jnp.bfloat16)
    gate_term = jnp.einsum(
        "sf,jsc->fjc", d_gate, rows4, preferred_element_type=jnp.float32
    ).astype(jnp.bfloat16).reshape(hidden_units, model_width)
    weight_grads = lax.psum_scatter(gate_term, "dp", scatter_dimension=1, tiled=True)
    grad_gate = weight_grads.astype(jnp.float32)[None]

    outs4 = jnp.concatenate([mixed4, input4], axis=2)
    slot_out = ring_reduce_scatter(outs4, "etp", shares).astype(jnp.bfloat16)
    back = lax.all_to_all(
        slot_out.reshape(experts, capacity, 2 * part), "expert", split_axis=0, concat_axis=0, tiled=True
    )
    token_out = back.reshape(slot_rows, 2 * part)[slot_index].reshape(tok_count, top_count, 2 * part)
    token_out = token_out.astype(jnp.float32)
    mixed = jnp.sum(route_weights[:, :, None] * token_out[:, :, :part], axis=1)
    grad_tokens = jnp.sum(token_out[:, :, part:], axis=1)
    return (mixed.astype(jnp.bfloat16), grad_tokens.astype(jnp.bfloat16), grad_gate)


def solution(mesh):
    in_specs = (
        P(("dp", "expert"), None),
        P(("dp", "expert"), None),
        P(("dp", "expert"), None),
        P(("dp", "expert"), None),
        P("expert", "etp", "dp"),
        P("expert", "etp", "dp"),
        P("expert", "etp", "dp"),
    )
    out_specs = (P(("dp", "expert"), "etp"), P(("dp", "expert"), "etp"), P("expert", "etp", "dp"))
    return jax.shard_map(
        on_device, mesh=mesh, in_specs=in_specs, out_specs=out_specs, check_vma=False
    )
```

```python
import jax
import jax.numpy as jnp
from jax import lax
from jax.sharding import PartitionSpec as P


def ring_gather(piece, axis, n, along=0):
    idx = lax.axis_index(axis)
    fwd = [(i, (i + 1) % n) for i in range(n)]
    bwd = [(i, (i - 1) % n) for i in range(n)]
    shape = list(piece.shape)
    shape.insert(along, n)
    out = jnp.zeros(shape, piece.dtype)
    put = lambda buf, val, at: lax.dynamic_update_index_in_dim(buf, val, at % n, along)
    out = put(out, piece, idx)
    left = right = piece
    half = n // 2
    for k in range(1, half):
        left = lax.ppermute(left, axis, fwd)
        right = lax.ppermute(right, axis, bwd)
        out = put(out, left, idx - k)
        out = put(out, right, idx + k)
    m = piece.shape[0] // 2
    first = lax.ppermute(left[:m], axis, fwd)
    second = lax.ppermute(right[m:], axis, bwd)
    return put(out, jnp.concatenate([first, second], axis=0), idx + half)


def ring_reduce_scatter(chunks, axis, n):
    idx = lax.axis_index(axis)
    fwd = [(i, (i + 1) % n) for i in range(n)]
    bwd = [(i, (i - 1) % n) for i in range(n)]
    pick = lambda at: lax.dynamic_index_in_dim(chunks, at % n, 0, keepdims=False).astype(jnp.float32)
    half = n // 2
    m = chunks.shape[1] // 2
    to_right = pick(idx + half)[:m]
    to_left = pick(idx - half)[m:]
    for k in range(2, half + 1):
        got_left = lax.ppermute(to_right.astype(chunks.dtype), axis, fwd).astype(jnp.float32)
        got_right = lax.ppermute(to_left.astype(chunks.dtype), axis, bwd).astype(jnp.float32)
        own_r = pick(idx + half - k + 1)
        own_l = pick(idx - half + k - 1)
        if k == 2:
            to_right = own_r.at[:m].add(got_left)
            to_left = own_l.at[m:].add(got_right)
        else:
            to_right = own_r + got_left
            to_left = own_l + got_right
    got_left = lax.ppermute(to_right.astype(chunks.dtype), axis, fwd).astype(jnp.float32)
    got_right = lax.ppermute(to_left.astype(chunks.dtype), axis, bwd).astype(jnp.float32)
    return pick(idx) + got_left + got_right


def on_device(tokens, cotangent, route_weights, expert_ids, w_gate, w_up, w_down):
    tok_count, model_width = tokens.shape
    top_count = expert_ids.shape[1]
    experts = lax.axis_size("expert")
    shares = lax.axis_size("etp")
    part = model_width // shares
    share_idx = lax.axis_index("etp")
    capacity = tok_count // experts * top_count + min(top_count, tok_count % experts)
    slot_rows = experts * capacity
    named_count = jnp.sum(
        (expert_ids[:, :, None] == jnp.arange(experts, dtype=jnp.int32)).astype(jnp.int32), axis=1
    )
    before = jnp.cumsum(named_count, axis=0) - named_count
    position = jnp.take_along_axis(before, expert_ids, axis=1)
    slot_index = (expert_ids * capacity + position).reshape(-1)

    tok_part = lax.dynamic_slice_in_dim(tokens, share_idx * part, part, axis=1)
    cot_part = lax.dynamic_slice_in_dim(cotangent, share_idx * part, part, axis=1)
    copies = jnp.broadcast_to(tok_part[:, None, :], (tok_count, top_count, part)).reshape(-1, part)
    scaled = (
        (route_weights[:, :, None] * cot_part[:, None, :].astype(jnp.float32))
        .astype(jnp.bfloat16)
        .reshape(-1, part)
    )
    empty_slots = jnp.zeros((slot_rows, part), jnp.bfloat16)

    def dispatch(values):
        send = empty_slots.at[slot_index].set(values).reshape(experts, capacity, part)
        recv = lax.all_to_all(send, "expert", split_axis=0, concat_axis=0, tiled=True)
        return ring_gather(recv.reshape(slot_rows, part), "etp", shares)

    rows4 = dispatch(copies)
    grads4 = dispatch(scaled)

    gate_full, up_full, down_full = (
        lax.all_gather(w_gate[0], "dp", axis=1, tiled=True),
        lax.all_gather(w_up[0], "dp", axis=1, tiled=True),
        ring_gather(w_down[0], "dp", lax.axis_size("dp"), along=1).reshape(w_down.shape[1], -1),
    )
    hidden_units = gate_full.shape[0]
    gate4 = gate_full.reshape(hidden_units, shares, part)
    up4 = up_full.reshape(hidden_units, shares, part)
    down4 = down_full.reshape(hidden_units, shares, part)

    gate_value = jnp.einsum("jsc,fjc->sf", rows4, gate4, preferred_element_type=jnp.float32)
    up_value = jnp.einsum("jsc,fjc->sf", rows4, up4, preferred_element_type=jnp.float32)
    sigmoid_gate = jax.nn.sigmoid(gate_value)
    active = gate_value * sigmoid_gate
    hidden = (active * up_value).astype(jnp.bfloat16)
    mixed4 = jnp.einsum("sf,fjc->jsc", hidden, down4, preferred_element_type=jnp.float32).astype(
        jnp.bfloat16
    )
    d_hidden = jnp.einsum("jsc,fjc->sf", grads4, down4, preferred_element_type=jnp.float32)
    d_gate = (
        d_hidden * up_value * sigmoid_gate * (1.0 + gate_value * (1.0 - sigmoid_gate))
    ).astype(jnp.bfloat16)
    d_up = (d_hidden * active).astype(jnp.bfloat16)
    input4 = (
        jnp.einsum("sf,fjc->jsc", d_gate, gate4, preferred_element_type=jnp.float32)
        + jnp.einsum("sf,fjc->jsc", d_up, up4, preferred_element_type=jnp.float32)
    ).astype(jnp.bfloat16)
    gate_term = jnp.einsum(
        "sf,jsc->fjc", d_gate, rows4, preferred_element_type=jnp.float32
    ).astype(jnp.bfloat16).reshape(hidden_units, model_width)
    weight_grads = lax.psum_scatter(gate_term, "dp", scatter_dimension=1, tiled=True)
    grad_gate = weight_grads.astype(jnp.float32)[None]

    def collect(outs4):
        slot_out = ring_reduce_scatter(outs4, "etp", shares).astype(jnp.bfloat16)
        back = lax.all_to_all(
            slot_out.reshape(experts, capacity, part), "expert", split_axis=0, concat_axis=0, tiled=True
        )
        token_out = back.reshape(slot_rows, part)[slot_index].reshape(tok_count, top_count, part)
        return token_out.astype(jnp.float32)

    mixed = jnp.sum(route_weights[:, :, None] * collect(mixed4), axis=1)
    grad_tokens = jnp.sum(collect(input4), axis=1)
    return (mixed.astype(jnp.bfloat16), grad_tokens.astype(jnp.bfloat16), grad_gate)


def solution(mesh):
    in_specs = (
        P(("dp", "expert"), None),
        P(("dp", "expert"), None),
        P(("dp", "expert"), None),
        P(("dp", "expert"), None),
        P("expert", "etp", "dp"),
        P("expert", "etp", "dp"),
        P("expert", "etp", "dp"),
    )
    out_specs = (P(("dp", "expert"), "etp"), P(("dp", "expert"), "etp"), P("expert", "etp", "dp"))
    return jax.shard_map(
        on_device, mesh=mesh, in_specs=in_specs, out_specs=out_specs, check_vma=False
    )
```

```python
import jax
import jax.numpy as jnp
from jax import lax
from jax.sharding import PartitionSpec as P


def ring_gather(piece, axis, n, along=0, tie=None):
    idx = lax.axis_index(axis)
    fwd = [(i, (i + 1) % n) for i in range(n)]
    bwd = [(i, (i - 1) % n) for i in range(n)]
    shape = list(piece.shape)
    shape.insert(along, n)
    out = jnp.zeros(shape, piece.dtype)
    put = lambda buf, val, at: lax.dynamic_update_index_in_dim(buf, val, at % n, along)
    out = put(out, piece, idx)
    left = right = piece
    half = n // 2
    for k in range(1, half):
        left = lax.ppermute(left, axis, fwd)
        right = lax.ppermute(right, axis, bwd)
        if k == 1 and tie is not None:
            left, right, tie = lax.optimization_barrier((left, right, tie))
        out = put(out, left, idx - k)
        out = put(out, right, idx + k)
    m = piece.shape[0] // 2
    first = lax.ppermute(left[:m], axis, fwd)
    second = lax.ppermute(right[m:], axis, bwd)
    out = put(out, jnp.concatenate([first, second], axis=0), idx + half)
    return out if tie is None else (out, tie)


def ring_reduce_scatter(chunks, axis, n):
    idx = lax.axis_index(axis)
    fwd = [(i, (i + 1) % n) for i in range(n)]
    bwd = [(i, (i - 1) % n) for i in range(n)]
    pick = lambda at: lax.dynamic_index_in_dim(chunks, at % n, 0, keepdims=False).astype(jnp.float32)
    half = n // 2
    m = chunks.shape[1] // 2
    to_right = pick(idx + half)[:m]
    to_left = pick(idx - half)[m:]
    for k in range(2, half + 1):
        got_left = lax.ppermute(to_right.astype(chunks.dtype), axis, fwd).astype(jnp.float32)
        got_right = lax.ppermute(to_left.astype(chunks.dtype), axis, bwd).astype(jnp.float32)
        own_r = pick(idx + half - k + 1)
        own_l = pick(idx - half + k - 1)
        if k == 2:
            to_right = own_r.at[:m].add(got_left)
            to_left = own_l.at[m:].add(got_right)
        else:
            to_right = own_r + got_left
            to_left = own_l + got_right
    got_left = lax.ppermute(to_right.astype(chunks.dtype), axis, fwd).astype(jnp.float32)
    got_right = lax.ppermute(to_left.astype(chunks.dtype), axis, bwd).astype(jnp.float32)
    return pick(idx) + got_left + got_right


def on_device(tokens, cotangent, route_weights, expert_ids, w_gate, w_up, w_down):
    tok_count, model_width = tokens.shape
    top_count = expert_ids.shape[1]
    experts = lax.axis_size("expert")
    shares = lax.axis_size("etp")
    part = model_width // shares
    share_idx = lax.axis_index("etp")
    capacity = tok_count // experts * top_count + min(top_count, tok_count % experts)
    slot_rows = experts * capacity
    named_count = jnp.sum(
        (expert_ids[:, :, None] == jnp.arange(experts, dtype=jnp.int32)).astype(jnp.int32), axis=1
    )
    before = jnp.cumsum(named_count, axis=0) - named_count
    position = jnp.take_along_axis(before, expert_ids, axis=1)
    slot_index = (expert_ids * capacity + position).reshape(-1)

    tok_part = lax.dynamic_slice_in_dim(tokens, share_idx * part, part, axis=1)
    cot_part = lax.dynamic_slice_in_dim(cotangent, share_idx * part, part, axis=1)
    copies = jnp.broadcast_to(tok_part[:, None, :], (tok_count, top_count, part))
    scaled = (route_weights[:, :, None] * cot_part[:, None, :].astype(jnp.float32)).astype(jnp.bfloat16)
    both = jnp.concatenate([copies, scaled], axis=2).reshape(-1, 2 * part)
    empty_slots = jnp.zeros((slot_rows, 2 * part), jnp.bfloat16)
    send = empty_slots.at[slot_index].set(both).reshape(experts, capacity, 2 * part)
    stacked = jnp.stack([w_gate[0], w_up[0], w_down[0]], axis=1)
    full, send = ring_gather(stacked, "dp", lax.axis_size("dp"), along=2, tie=send)
    gate_full, up_full, down_full = (
        full[:, i].reshape(w_gate.shape[1], model_width) for i in range(3)
    )
    recv = lax.all_to_all(send, "expert", split_axis=0, concat_axis=0, tiled=True)
    recv = recv.reshape(1, slot_rows, 2 * part)
    gathered = lax.all_gather(recv[0], "etp", axis=0, tiled=False)
    rows4 = gathered[:, :, :part]
    grads4 = gathered[:, :, part:]

    hidden_units = gate_full.shape[0]
    gate4 = gate_full.reshape(hidden_units, shares, part)
    up4 = up_full.reshape(hidden_units, shares, part)
    down4 = down_full.reshape(hidden_units, shares, part)

    gate_value = jnp.einsum("jsc,fjc->sf", rows4, gate4, preferred_element_type=jnp.float32)
    up_value = jnp.einsum("jsc,fjc->sf", rows4, up4, preferred_element_type=jnp.float32)
    sigmoid_gate = jax.nn.sigmoid(gate_value)
    active = gate_value * sigmoid_gate
    hidden = (active * up_value).astype(jnp.bfloat16)
    mixed4 = jnp.einsum("sf,fjc->jsc", hidden, down4, preferred_element_type=jnp.float32).astype(
        jnp.bfloat16
    )
    d_hidden = jnp.einsum("jsc,fjc->sf", grads4, down4, preferred_element_type=jnp.float32)
    d_gate = (
        d_hidden * up_value * sigmoid_gate * (1.0 + gate_value * (1.0 - sigmoid_gate))
    ).astype(jnp.bfloat16)
    d_up = (d_hidden * active).astype(jnp.bfloat16)
    input4 = (
        jnp.einsum("sf,fjc->jsc", d_gate, gate4, preferred_element_type=jnp.float32)
        + jnp.einsum("sf,fjc->jsc", d_up, up4, preferred_element_type=jnp.float32)
    ).astype(jnp.bfloat16)
    gate_term = jnp.einsum(
        "sf,jsc->fjc", d_gate, rows4, preferred_element_type=jnp.float32
    ).astype(jnp.bfloat16).reshape(hidden_units, model_width)
    weight_grads = lax.psum_scatter(gate_term, "dp", scatter_dimension=1, tiled=True)
    grad_gate = weight_grads.astype(jnp.float32)[None]

    outs4 = jnp.concatenate([mixed4, input4], axis=2)
    slot_out = ring_reduce_scatter(outs4, "etp", shares).astype(jnp.bfloat16)
    back = lax.all_to_all(
        slot_out.reshape(experts, capacity, 2 * part), "expert", split_axis=0, concat_axis=0, tiled=True
    )
    token_out = back.reshape(slot_rows, 2 * part)[slot_index].reshape(tok_count, top_count, 2 * part)
    token_out = token_out.astype(jnp.float32)
    mixed = jnp.sum(route_weights[:, :, None] * token_out[:, :, :part], axis=1)
    grad_tokens = jnp.sum(token_out[:, :, part:], axis=1)
    return (mixed.astype(jnp.bfloat16), grad_tokens.astype(jnp.bfloat16), grad_gate)


def solution(mesh):
    in_specs = (
        P(("dp", "expert"), None),
        P(("dp", "expert"), None),
        P(("dp", "expert"), None),
        P(("dp", "expert"), None),
        P("expert", "etp", "dp"),
        P("expert", "etp", "dp"),
        P("expert", "etp", "dp"),
    )
    out_specs = (P(("dp", "expert"), "etp"), P(("dp", "expert"), "etp"), P("expert", "etp", "dp"))
    return jax.shard_map(
        on_device, mesh=mesh, in_specs=in_specs, out_specs=out_specs, check_vma=False
    )
```

```python
import jax
import jax.numpy as jnp
from jax import lax
from jax.sharding import PartitionSpec as P


def ring_gather(piece, axis, n, along=0):
    idx = lax.axis_index(axis)
    fwd = [(i, (i + 1) % n) for i in range(n)]
    bwd = [(i, (i - 1) % n) for i in range(n)]
    shape = list(piece.shape)
    shape.insert(along, n)
    out = jnp.zeros(shape, piece.dtype)
    put = lambda buf, val, at: lax.dynamic_update_index_in_dim(buf, val, at % n, along)
    out = put(out, piece, idx)
    left = right = piece
    half = n // 2
    for k in range(1, half):
        left = lax.ppermute(left, axis, fwd)
        right = lax.ppermute(right, axis, bwd)
        out = put(out, left, idx - k)
        out = put(out, right, idx + k)
    m = piece.shape[0] // 2
    first = lax.ppermute(left[:m], axis, fwd)
    second = lax.ppermute(right[m:], axis, bwd)
    return put(out, jnp.concatenate([first, second], axis=0), idx + half)


def ring_reduce_scatter(chunks, axis, n):
    idx = lax.axis_index(axis)
    fwd = [(i, (i + 1) % n) for i in range(n)]
    bwd = [(i, (i - 1) % n) for i in range(n)]
    pick = lambda at: lax.dynamic_index_in_dim(chunks, at % n, 0, keepdims=False).astype(jnp.float32)
    half = n // 2
    m = chunks.shape[1] // 2
    to_right = pick(idx + half)[:m]
    to_left = pick(idx - half)[m:]
    for k in range(2, half + 1):
        got_left = lax.ppermute(to_right.astype(chunks.dtype), axis, fwd).astype(jnp.float32)
        got_right = lax.ppermute(to_left.astype(chunks.dtype), axis, bwd).astype(jnp.float32)
        own_r = pick(idx + half - k + 1)
        own_l = pick(idx - half + k - 1)
        if k == 2:
            to_right = own_r.at[:m].add(got_left)
            to_left = own_l.at[m:].add(got_right)
        else:
            to_right = own_r + got_left
            to_left = own_l + got_right
    got_left = lax.ppermute(to_right.astype(chunks.dtype), axis, fwd).astype(jnp.float32)
    got_right = lax.ppermute(to_left.astype(chunks.dtype), axis, bwd).astype(jnp.float32)
    return pick(idx) + got_left + got_right


def on_device(tokens, cotangent, route_weights, expert_ids, w_gate, w_up, w_down):
    tok_count, model_width = tokens.shape
    top_count = expert_ids.shape[1]
    experts = lax.axis_size("expert")
    shares = lax.axis_size("etp")
    part = model_width // shares
    share_idx = lax.axis_index("etp")
    capacity = tok_count // experts * top_count + min(top_count, tok_count % experts)
    slot_rows = experts * capacity
    named_count = jnp.sum(
        (expert_ids[:, :, None] == jnp.arange(experts, dtype=jnp.int32)).astype(jnp.int32), axis=1
    )
    before = jnp.cumsum(named_count, axis=0) - named_count
    position = jnp.take_along_axis(before, expert_ids, axis=1)
    slot_index = (expert_ids * capacity + position).reshape(-1)

    tok_part = lax.dynamic_slice_in_dim(tokens, share_idx * part, part, axis=1)
    cot_part = lax.dynamic_slice_in_dim(cotangent, share_idx * part, part, axis=1)
    copies = jnp.broadcast_to(tok_part[:, None, :], (tok_count, top_count, part))
    scaled = (route_weights[:, :, None] * cot_part[:, None, :].astype(jnp.float32)).astype(jnp.bfloat16)
    both = jnp.concatenate([copies, scaled], axis=2).reshape(-1, 2 * part)
    empty_slots = jnp.zeros((slot_rows, 2 * part), jnp.bfloat16)
    send = empty_slots.at[slot_index].set(both).reshape(experts, capacity, 2 * part)
    recv = lax.all_to_all(send, "expert", split_axis=0, concat_axis=0, tiled=True)
    recv = recv.reshape(1, slot_rows, 2 * part)
    gathered = ring_gather(recv[0], "etp", shares)
    rows4 = gathered[:, :, :part]
    grads4 = gathered[:, :, part:]

    gate_full, up_full, down_full = (
        *lax.all_gather(jnp.stack([w_gate[0], w_up[0]]), "dp", axis=2, tiled=True),
        ring_gather(w_down[0], "dp", lax.axis_size("dp"), along=1).reshape(w_down.shape[1], -1),
    )
    hidden_units = gate_full.shape[0]
    gate4 = gate_full.reshape(hidden_units, shares, part)
    up4 = up_full.reshape(hidden_units, shares, part)
    down4 = down_full.reshape(hidden_units, shares, part)

    gate_value = jnp.einsum("jsc,fjc->sf", rows4, gate4, preferred_element_type=jnp.float32)
    up_value = jnp.einsum("jsc,fjc->sf", rows4, up4, preferred_element_type=jnp.float32)
    sigmoid_gate = jax.nn.sigmoid(gate_value)
    active = gate_value * sigmoid_gate
    hidden = (active * up_value).astype(jnp.bfloat16)
    mixed4 = jnp.einsum("sf,fjc->jsc", hidden, down4, preferred_element_type=jnp.float32).astype(
        jnp.bfloat16
    )
    d_hidden = jnp.einsum("jsc,fjc->sf", grads4, down4, preferred_element_type=jnp.float32)
    d_gate = (
        d_hidden * up_value * sigmoid_gate * (1.0 + gate_value * (1.0 - sigmoid_gate))
    ).astype(jnp.bfloat16)
    d_up = (d_hidden * active).astype(jnp.bfloat16)
    input4 = (
        jnp.einsum("sf,fjc->jsc", d_gate, gate4, preferred_element_type=jnp.float32)
        + jnp.einsum("sf,fjc->jsc", d_up, up4, preferred_element_type=jnp.float32)
    ).astype(jnp.bfloat16)
    gate_term = jnp.einsum(
        "sf,jsc->fjc", d_gate, rows4, preferred_element_type=jnp.float32
    ).astype(jnp.bfloat16).reshape(hidden_units, model_width)
    weight_grads = lax.psum_scatter(gate_term, "dp", scatter_dimension=1, tiled=True)
    grad_gate = weight_grads.astype(jnp.float32)[None]

    outs4 = jnp.concatenate([mixed4, input4], axis=2)
    slot_out = ring_reduce_scatter(outs4, "etp", shares).astype(jnp.bfloat16)
    back = lax.all_to_all(
        slot_out.reshape(experts, capacity, 2 * part), "expert", split_axis=0, concat_axis=0, tiled=True
    )
    token_out = back.reshape(slot_rows, 2 * part)[slot_index].reshape(tok_count, top_count, 2 * part)
    token_out = token_out.astype(jnp.float32)
    mixed = jnp.sum(route_weights[:, :, None] * token_out[:, :, :part], axis=1)
    grad_tokens = jnp.sum(token_out[:, :, part:], axis=1)
    return (mixed.astype(jnp.bfloat16), grad_tokens.astype(jnp.bfloat16), grad_gate)


def solution(mesh):
    in_specs = (
        P(("dp", "expert"), None),
        P(("dp", "expert"), None),
        P(("dp", "expert"), None),
        P(("dp", "expert"), None),
        P("expert", "etp", "dp"),
        P("expert", "etp", "dp"),
        P("expert", "etp", "dp"),
    )
    out_specs = (P(("dp", "expert"), "etp"), P(("dp", "expert"), "etp"), P("expert", "etp", "dp"))
    return jax.shard_map(
        on_device, mesh=mesh, in_specs=in_specs, out_specs=out_specs, check_vma=False
    )
```

```python
import jax
import jax.numpy as jnp
from jax import lax
from jax.sharding import PartitionSpec as P


def ring_gather(piece, axis, n, along=0):
    idx = lax.axis_index(axis)
    fwd = [(i, (i + 1) % n) for i in range(n)]
    bwd = [(i, (i - 1) % n) for i in range(n)]
    shape = list(piece.shape)
    shape.insert(along, n)
    out = jnp.zeros(shape, piece.dtype)
    put = lambda buf, val, at: lax.dynamic_update_index_in_dim(buf, val, at % n, along)
    out = put(out, piece, idx)
    left = right = piece
    half = n // 2
    for k in range(1, half):
        left = lax.ppermute(left, axis, fwd)
        right = lax.ppermute(right, axis, bwd)
        out = put(out, left, idx - k)
        out = put(out, right, idx + k)
    m = piece.shape[0] // 2
    first = lax.ppermute(left[:m], axis, fwd)
    second = lax.ppermute(right[m:], axis, bwd)
    return put(out, jnp.concatenate([first, second], axis=0), idx + half)


def ring_reduce_scatter(chunks, axis, n):
    idx = lax.axis_index(axis)
    fwd = [(i, (i + 1) % n) for i in range(n)]
    bwd = [(i, (i - 1) % n) for i in range(n)]
    pick = lambda at: lax.dynamic_index_in_dim(chunks, at % n, 0, keepdims=False).astype(jnp.float32)
    half = n // 2
    m = chunks.shape[1] // 2
    to_right = pick(idx + half)[:m]
    to_left = pick(idx - half)[m:]
    for k in range(2, half + 1):
        got_left = lax.ppermute(to_right.astype(chunks.dtype), axis, fwd).astype(jnp.float32)
        got_right = lax.ppermute(to_left.astype(chunks.dtype), axis, bwd).astype(jnp.float32)
        own_r = pick(idx + half - k + 1)
        own_l = pick(idx - half + k - 1)
        if k == 2:
            to_right = own_r.at[:m].add(got_left)
            to_left = own_l.at[m:].add(got_right)
        else:
            to_right = own_r + got_left
            to_left = own_l + got_right
    got_left = lax.ppermute(to_right.astype(chunks.dtype), axis, fwd).astype(jnp.float32)
    got_right = lax.ppermute(to_left.astype(chunks.dtype), axis, bwd).astype(jnp.float32)
    return pick(idx) + got_left + got_right


def on_device(tokens, cotangent, route_weights, expert_ids, w_gate, w_up, w_down):
    tok_count, model_width = tokens.shape
    top_count = expert_ids.shape[1]
    experts = lax.axis_size("expert")
    shares = lax.axis_size("etp")
    part = model_width // shares
    share_idx = lax.axis_index("etp")
    capacity = tok_count // experts * top_count + min(top_count, tok_count % experts)
    slot_rows = experts * capacity
    named_count = jnp.sum(
        (expert_ids[:, :, None] == jnp.arange(experts, dtype=jnp.int32)).astype(jnp.int32), axis=1
    )
    before = jnp.cumsum(named_count, axis=0) - named_count
    position = jnp.take_along_axis(before, expert_ids, axis=1)
    slot_index = (expert_ids * capacity + position).reshape(-1)

    tok_part = lax.dynamic_slice_in_dim(tokens, share_idx * part, part, axis=1)
    cot_part = lax.dynamic_slice_in_dim(cotangent, share_idx * part, part, axis=1)
    copies = jnp.broadcast_to(tok_part[:, None, :], (tok_count, top_count, part))
    scaled = (route_weights[:, :, None] * cot_part[:, None, :].astype(jnp.float32)).astype(jnp.bfloat16)
    both = jnp.concatenate([copies, scaled], axis=2).reshape(-1, 2 * part)
    empty_slots = jnp.zeros((slot_rows, 2 * part), jnp.bfloat16)
    send = empty_slots.at[slot_index].set(both).reshape(experts, capacity, 2 * part)
    recv = lax.all_to_all(send, "expert", split_axis=0, concat_axis=0, tiled=True)
    recv = recv.reshape(1, slot_rows, 2 * part)
    gathered = ring_gather(recv[0], "etp", shares)
    rows4 = gathered[:, :, :part]
    grads4 = gathered[:, :, part:]

    gate_full = lax.all_gather(w_gate[0], "dp", axis=1, tiled=True)
    pair = ring_gather(jnp.stack([w_up[0], w_down[0]], axis=1), "dp", lax.axis_size("dp"), along=2)
    up_full, down_full = (pair[:, i].reshape(w_up.shape[1], model_width) for i in range(2))
    hidden_units = gate_full.shape[0]
    gate4 = gate_full.reshape(hidden_units, shares, part)
    up4 = up_full.reshape(hidden_units, shares, part)
    down4 = down_full.reshape(hidden_units, shares, part)

    gate_value = jnp.einsum("jsc,fjc->sf", rows4, gate4, preferred_element_type=jnp.float32)
    up_value = jnp.einsum("jsc,fjc->sf", rows4, up4, preferred_element_type=jnp.float32)
    sigmoid_gate = jax.nn.sigmoid(gate_value)
    active = gate_value * sigmoid_gate
    hidden = (active * up_value).astype(jnp.bfloat16)
    mixed4 = jnp.einsum("sf,fjc->jsc", hidden, down4, preferred_element_type=jnp.float32).astype(
        jnp.bfloat16
    )
    d_hidden = jnp.einsum("jsc,fjc->sf", grads4, down4, preferred_element_type=jnp.float32)
    d_gate = (
        d_hidden * up_value * sigmoid_gate * (1.0 + gate_value * (1.0 - sigmoid_gate))
    ).astype(jnp.bfloat16)
    d_up = (d_hidden * active).astype(jnp.bfloat16)
    input4 = (
        jnp.einsum("sf,fjc->jsc", d_gate, gate4, preferred_element_type=jnp.float32)
        + jnp.einsum("sf,fjc->jsc", d_up, up4, preferred_element_type=jnp.float32)
    ).astype(jnp.bfloat16)
    gate_term = jnp.einsum(
        "sf,jsc->fjc", d_gate, rows4, preferred_element_type=jnp.float32
    ).astype(jnp.bfloat16).reshape(hidden_units, model_width)
    weight_grads = lax.psum_scatter(gate_term, "dp", scatter_dimension=1, tiled=True)
    grad_gate = weight_grads.astype(jnp.float32)[None]

    outs4 = jnp.concatenate([mixed4, input4], axis=2)
    slot_out = ring_reduce_scatter(outs4, "etp", shares).astype(jnp.bfloat16)
    back = lax.all_to_all(
        slot_out.reshape(experts, capacity, 2 * part), "expert", split_axis=0, concat_axis=0, tiled=True
    )
    token_out = back.reshape(slot_rows, 2 * part)[slot_index].reshape(tok_count, top_count, 2 * part)
    token_out = token_out.astype(jnp.float32)
    mixed = jnp.sum(route_weights[:, :, None] * token_out[:, :, :part], axis=1)
    grad_tokens = jnp.sum(token_out[:, :, part:], axis=1)
    return (mixed.astype(jnp.bfloat16), grad_tokens.astype(jnp.bfloat16), grad_gate)


def solution(mesh):
    in_specs = (
        P(("dp", "expert"), None),
        P(("dp", "expert"), None),
        P(("dp", "expert"), None),
        P(("dp", "expert"), None),
        P("expert", "etp", "dp"),
        P("expert", "etp", "dp"),
        P("expert", "etp", "dp"),
    )
    out_specs = (P(("dp", "expert"), "etp"), P(("dp", "expert"), "etp"), P("expert", "etp", "dp"))
    return jax.shard_map(
        on_device, mesh=mesh, in_specs=in_specs, out_specs=out_specs, check_vma=False
    )
```

```python
import jax
import jax.numpy as jnp
from jax import lax
from jax.sharding import PartitionSpec as P


def ring_reduce_scatter(chunks, axis, n):
    idx = lax.axis_index(axis)
    fwd = [(i, (i + 1) % n) for i in range(n)]
    bwd = [(i, (i - 1) % n) for i in range(n)]
    pick = lambda at: lax.dynamic_index_in_dim(chunks, at % n, 0, keepdims=False).astype(jnp.float32)
    half = n // 2
    m = chunks.shape[1] // 2
    to_right = pick(idx + half)[:m]
    to_left = pick(idx - half)[m:]
    for k in range(2, half + 1):
        got_left = lax.ppermute(to_right.astype(chunks.dtype), axis, fwd).astype(jnp.float32)
        got_right = lax.ppermute(to_left.astype(chunks.dtype), axis, bwd).astype(jnp.float32)
        own_r = pick(idx + half - k + 1)
        own_l = pick(idx - half + k - 1)
        if k == 2:
            to_right = own_r.at[:m].add(got_left)
            to_left = own_l.at[m:].add(got_right)
        else:
            to_right = own_r + got_left
            to_left = own_l + got_right
    got_left = lax.ppermute(to_right.astype(chunks.dtype), axis, fwd).astype(jnp.float32)
    got_right = lax.ppermute(to_left.astype(chunks.dtype), axis, bwd).astype(jnp.float32)
    return pick(idx) + got_left + got_right


class Ring:
    def __init__(self, piece, axis, n, along=0):
        self.piece, self.axis, self.n, self.along = piece, axis, n, along
        self.left = self.right = piece
        self.hop = 0
        self.got = []

    def active(self):
        return self.hop < self.n // 2

    def step(self):
        n, half = self.n, self.n // 2
        fwd = [(i, (i + 1) % n) for i in range(n)]
        bwd = [(i, (i - 1) % n) for i in range(n)]
        self.hop += 1
        if self.hop < half:
            self.left = lax.ppermute(self.left, self.axis, fwd)
            self.right = lax.ppermute(self.right, self.axis, bwd)
        else:
            m = self.piece.shape[0] // 2
            self.left = lax.ppermute(self.left[:m], self.axis, fwd)
            self.right = lax.ppermute(self.right[m:], self.axis, bwd)

    def record(self):
        if self.hop < self.n // 2:
            self.got += [(-self.hop, self.left), (self.hop, self.right)]
        else:
            self.got.append((self.hop, jnp.concatenate([self.left, self.right], axis=0)))

    def result(self):
        idx = lax.axis_index(self.axis)
        shape = list(self.piece.shape)
        shape.insert(self.along, self.n)
        out = jnp.zeros(shape, self.piece.dtype)
        for offset, val in [(0, self.piece)] + self.got:
            out = lax.dynamic_update_index_in_dim(out, val, (idx + offset) % self.n, self.along)
        return out


def lockstep(rings):
    live = [r for r in rings if r.active()]
    for r in live:
        r.step()
    held = lax.optimization_barrier(tuple((r.left, r.right) for r in live))
    for r, (left, right) in zip(live, held):
        r.left, r.right = left, right
        r.record()


def on_device(tokens, cotangent, route_weights, expert_ids, w_gate, w_up, w_down):
    tok_count, model_width = tokens.shape
    top_count = expert_ids.shape[1]
    experts = lax.axis_size("expert")
    shares = lax.axis_size("etp")
    part = model_width // shares
    share_idx = lax.axis_index("etp")
    capacity = tok_count // experts * top_count + min(top_count, tok_count % experts)
    slot_rows = experts * capacity
    named_count = jnp.sum(
        (expert_ids[:, :, None] == jnp.arange(experts, dtype=jnp.int32)).astype(jnp.int32), axis=1
    )
    before = jnp.cumsum(named_count, axis=0) - named_count
    position = jnp.take_along_axis(before, expert_ids, axis=1)
    slot_index = (expert_ids * capacity + position).reshape(-1)

    tok_part = lax.dynamic_slice_in_dim(tokens, share_idx * part, part, axis=1)
    cot_part = lax.dynamic_slice_in_dim(cotangent, share_idx * part, part, axis=1)
    copies = jnp.broadcast_to(tok_part[:, None, :], (tok_count, top_count, part))
    scaled = (route_weights[:, :, None] * cot_part[:, None, :].astype(jnp.float32)).astype(jnp.bfloat16)
    both = jnp.concatenate([copies, scaled], axis=2).reshape(-1, 2 * part)
    empty_slots = jnp.zeros((slot_rows, 2 * part), jnp.bfloat16)
    send = empty_slots.at[slot_index].set(both).reshape(experts, capacity, 2 * part)
    recv = lax.all_to_all(send, "expert", split_axis=0, concat_axis=0, tiled=True)

    gate_full = lax.all_gather(w_gate[0], "dp", axis=1, tiled=True)
    weights = Ring(jnp.stack([w_up[0], w_down[0]], axis=1), "dp", lax.axis_size("dp"), along=2)
    lockstep([weights])
    weights.left, weights.right, recv = lax.optimization_barrier((weights.left, weights.right, recv))
    rows = Ring(recv.reshape(slot_rows, 2 * part), "etp", shares)
    while weights.active() or rows.active():
        lockstep([weights, rows])
    pair = weights.result()
    up_full, down_full = (pair[:, i].reshape(w_up.shape[1], model_width) for i in range(2))
    gathered = rows.result()
    rows4 = gathered[:, :, :part]
    grads4 = gathered[:, :, part:]

    hidden_units = gate_full.shape[0]
    gate4 = gate_full.reshape(hidden_units, shares, part)
    up4 = up_full.reshape(hidden_units, shares, part)
    down4 = down_full.reshape(hidden_units, shares, part)

    gate_value = jnp.einsum("jsc,fjc->sf", rows4, gate4, preferred_element_type=jnp.float32)
    up_value = jnp.einsum("jsc,fjc->sf", rows4, up4, preferred_element_type=jnp.float32)
    sigmoid_gate = jax.nn.sigmoid(gate_value)
    active = gate_value * sigmoid_gate
    hidden = (active * up_value).astype(jnp.bfloat16)
    mixed4 = jnp.einsum("sf,fjc->jsc", hidden, down4, preferred_element_type=jnp.float32).astype(
        jnp.bfloat16
    )
    d_hidden = jnp.einsum("jsc,fjc->sf", grads4, down4, preferred_element_type=jnp.float32)
    d_gate = (
        d_hidden * up_value * sigmoid_gate * (1.0 + gate_value * (1.0 - sigmoid_gate))
    ).astype(jnp.bfloat16)
    d_up = (d_hidden * active).astype(jnp.bfloat16)
    input4 = (
        jnp.einsum("sf,fjc->jsc", d_gate, gate4, preferred_element_type=jnp.float32)
        + jnp.einsum("sf,fjc->jsc", d_up, up4, preferred_element_type=jnp.float32)
    ).astype(jnp.bfloat16)
    gate_term = jnp.einsum(
        "sf,jsc->fjc", d_gate, rows4, preferred_element_type=jnp.float32
    ).astype(jnp.bfloat16).reshape(hidden_units, model_width)
    weight_grads = lax.psum_scatter(gate_term, "dp", scatter_dimension=1, tiled=True)
    grad_gate = weight_grads.astype(jnp.float32)[None]

    outs4 = jnp.concatenate([mixed4, input4], axis=2)
    slot_out = ring_reduce_scatter(outs4, "etp", shares).astype(jnp.bfloat16)
    back = lax.all_to_all(
        slot_out.reshape(experts, capacity, 2 * part), "expert", split_axis=0, concat_axis=0, tiled=True
    )
    token_out = back.reshape(slot_rows, 2 * part)[slot_index].reshape(tok_count, top_count, 2 * part)
    token_out = token_out.astype(jnp.float32)
    mixed = jnp.sum(route_weights[:, :, None] * token_out[:, :, :part], axis=1)
    grad_tokens = jnp.sum(token_out[:, :, part:], axis=1)
    return (mixed.astype(jnp.bfloat16), grad_tokens.astype(jnp.bfloat16), grad_gate)


def solution(mesh):
    in_specs = (
        P(("dp", "expert"), None),
        P(("dp", "expert"), None),
        P(("dp", "expert"), None),
        P(("dp", "expert"), None),
        P("expert", "etp", "dp"),
        P("expert", "etp", "dp"),
        P("expert", "etp", "dp"),
    )
    out_specs = (P(("dp", "expert"), "etp"), P(("dp", "expert"), "etp"), P("expert", "etp", "dp"))
    return jax.shard_map(
        on_device, mesh=mesh, in_specs=in_specs, out_specs=out_specs, check_vma=False
    )
```

```python
import jax
import jax.numpy as jnp
from jax import lax
from jax.sharding import PartitionSpec as P


def ring_reduce_scatter(chunks, axis, n):
    idx = lax.axis_index(axis)
    fwd = [(i, (i + 1) % n) for i in range(n)]
    bwd = [(i, (i - 1) % n) for i in range(n)]
    pick = lambda at: lax.dynamic_index_in_dim(chunks, at % n, 0, keepdims=False).astype(jnp.float32)
    half = n // 2
    m = chunks.shape[1] // 2
    to_right = pick(idx + half)[:m]
    to_left = pick(idx - half)[m:]
    for k in range(2, half + 1):
        got_left = lax.ppermute(to_right.astype(chunks.dtype), axis, fwd).astype(jnp.float32)
        got_right = lax.ppermute(to_left.astype(chunks.dtype), axis, bwd).astype(jnp.float32)
        own_r = pick(idx + half - k + 1)
        own_l = pick(idx - half + k - 1)
        if k == 2:
            to_right = own_r.at[:m].add(got_left)
            to_left = own_l.at[m:].add(got_right)
        else:
            to_right = own_r + got_left
            to_left = own_l + got_right
    got_left = lax.ppermute(to_right.astype(chunks.dtype), axis, fwd).astype(jnp.float32)
    got_right = lax.ppermute(to_left.astype(chunks.dtype), axis, bwd).astype(jnp.float32)
    return pick(idx) + got_left + got_right


class Ring:
    def __init__(self, piece, axis, n, along=0):
        self.piece, self.axis, self.n, self.along = piece, axis, n, along
        self.left = self.right = piece
        self.hop = 0
        self.got = []

    def active(self):
        return self.hop < self.n // 2

    def step(self):
        n, half = self.n, self.n // 2
        fwd = [(i, (i + 1) % n) for i in range(n)]
        bwd = [(i, (i - 1) % n) for i in range(n)]
        self.hop += 1
        if self.hop < half:
            self.left = lax.ppermute(self.left, self.axis, fwd)
            self.right = lax.ppermute(self.right, self.axis, bwd)
        else:
            m = self.piece.shape[0] // 2
            self.left = lax.ppermute(self.left[:m], self.axis, fwd)
            self.right = lax.ppermute(self.right[m:], self.axis, bwd)

    def record(self):
        if self.hop < self.n // 2:
            self.got += [(-self.hop, self.left), (self.hop, self.right)]
        else:
            self.got.append((self.hop, jnp.concatenate([self.left, self.right], axis=0)))

    def result(self):
        idx = lax.axis_index(self.axis)
        shape = list(self.piece.shape)
        shape.insert(self.along, self.n)
        out = jnp.zeros(shape, self.piece.dtype)
        for offset, val in [(0, self.piece)] + self.got:
            out = lax.dynamic_update_index_in_dim(out, val, (idx + offset) % self.n, self.along)
        return out


def lockstep(rings):
    live = [r for r in rings if r.active()]
    for r in live:
        r.step()
    held = lax.optimization_barrier(tuple((r.left, r.right) for r in live))
    for r, (left, right) in zip(live, held):
        r.left, r.right = left, right
        r.record()


def on_device(tokens, cotangent, route_weights, expert_ids, w_gate, w_up, w_down):
    tok_count, model_width = tokens.shape
    top_count = expert_ids.shape[1]
    experts = lax.axis_size("expert")
    shares = lax.axis_size("etp")
    part = model_width // shares
    share_idx = lax.axis_index("etp")
    capacity = tok_count // experts * top_count + min(top_count, tok_count % experts)
    slot_rows = experts * capacity
    named_count = jnp.sum(
        (expert_ids[:, :, None] == jnp.arange(experts, dtype=jnp.int32)).astype(jnp.int32), axis=1
    )
    before = jnp.cumsum(named_count, axis=0) - named_count
    position = jnp.take_along_axis(before, expert_ids, axis=1)
    slot_index = (expert_ids * capacity + position).reshape(-1)

    tok_part = lax.dynamic_slice_in_dim(tokens, share_idx * part, part, axis=1)
    cot_part = lax.dynamic_slice_in_dim(cotangent, share_idx * part, part, axis=1)
    copies = jnp.broadcast_to(tok_part[:, None, :], (tok_count, top_count, part))
    scaled = (route_weights[:, :, None] * cot_part[:, None, :].astype(jnp.float32)).astype(jnp.bfloat16)
    both = jnp.concatenate([copies, scaled], axis=2).reshape(-1, 2 * part)
    empty_slots = jnp.zeros((slot_rows, 2 * part), jnp.bfloat16)
    send = empty_slots.at[slot_index].set(both).reshape(experts, capacity, 2 * part)
    recv = lax.all_to_all(send, "expert", split_axis=0, concat_axis=0, tiled=True)

    weights = Ring(jnp.stack([w_gate[0], w_up[0], w_down[0]], axis=1), "dp", lax.axis_size("dp"), along=2)
    lockstep([weights])
    weights.left, weights.right, recv = lax.optimization_barrier((weights.left, weights.right, recv))
    rows = Ring(recv.reshape(slot_rows, 2 * part), "etp", shares)
    while weights.active() or rows.active():
        lockstep([weights, rows])
    full = weights.result()
    gate_full, up_full, down_full = (full[:, i].reshape(w_up.shape[1], model_width) for i in range(3))
    gathered = rows.result()
    rows4 = gathered[:, :, :part]
    grads4 = gathered[:, :, part:]

    hidden_units = gate_full.shape[0]
    gate4 = gate_full.reshape(hidden_units, shares, part)
    up4 = up_full.reshape(hidden_units, shares, part)
    down4 = down_full.reshape(hidden_units, shares, part)

    gate_value = jnp.einsum("jsc,fjc->sf", rows4, gate4, preferred_element_type=jnp.float32)
    up_value = jnp.einsum("jsc,fjc->sf", rows4, up4, preferred_element_type=jnp.float32)
    sigmoid_gate = jax.nn.sigmoid(gate_value)
    active = gate_value * sigmoid_gate
    hidden = (active * up_value).astype(jnp.bfloat16)
    mixed4 = jnp.einsum("sf,fjc->jsc", hidden, down4, preferred_element_type=jnp.float32).astype(
        jnp.bfloat16
    )
    d_hidden = jnp.einsum("jsc,fjc->sf", grads4, down4, preferred_element_type=jnp.float32)
    d_gate = (
        d_hidden * up_value * sigmoid_gate * (1.0 + gate_value * (1.0 - sigmoid_gate))
    ).astype(jnp.bfloat16)
    d_up = (d_hidden * active).astype(jnp.bfloat16)
    input4 = (
        jnp.einsum("sf,fjc->jsc", d_gate, gate4, preferred_element_type=jnp.float32)
        + jnp.einsum("sf,fjc->jsc", d_up, up4, preferred_element_type=jnp.float32)
    ).astype(jnp.bfloat16)
    gate_term = jnp.einsum(
        "sf,jsc->fjc", d_gate, rows4, preferred_element_type=jnp.float32
    ).astype(jnp.bfloat16).reshape(hidden_units, model_width)
    groups = lax.axis_size("dp")
    term_chunks = gate_term.reshape(hidden_units, groups, model_width // groups).transpose(1, 0, 2)
    grad_gate = ring_reduce_scatter(term_chunks, "dp", groups)[None]

    outs4 = jnp.concatenate([mixed4, input4], axis=2)
    slot_out = ring_reduce_scatter(outs4, "etp", shares).astype(jnp.bfloat16)
    back = lax.all_to_all(
        slot_out.reshape(experts, capacity, 2 * part), "expert", split_axis=0, concat_axis=0, tiled=True
    )
    token_out = back.reshape(slot_rows, 2 * part)[slot_index].reshape(tok_count, top_count, 2 * part)
    token_out = token_out.astype(jnp.float32)
    mixed = jnp.sum(route_weights[:, :, None] * token_out[:, :, :part], axis=1)
    grad_tokens = jnp.sum(token_out[:, :, part:], axis=1)
    return (mixed.astype(jnp.bfloat16), grad_tokens.astype(jnp.bfloat16), grad_gate)


def solution(mesh):
    in_specs = (
        P(("dp", "expert"), None),
        P(("dp", "expert"), None),
        P(("dp", "expert"), None),
        P(("dp", "expert"), None),
        P("expert", "etp", "dp"),
        P("expert", "etp", "dp"),
        P("expert", "etp", "dp"),
    )
    out_specs = (P(("dp", "expert"), "etp"), P(("dp", "expert"), "etp"), P("expert", "etp", "dp"))
    return jax.shard_map(
        on_device, mesh=mesh, in_specs=in_specs, out_specs=out_specs, check_vma=False
    )
```

```python
import jax
import jax.numpy as jnp
from jax import lax
from jax.sharding import PartitionSpec as P


class Ring:
    def __init__(self, piece, axis, n, along=0):
        self.piece, self.axis, self.n, self.along = piece, axis, n, along
        self.left = self.right = piece
        self.hop = 0
        self.got = []

    def active(self):
        return self.hop < self.n // 2

    def step(self):
        n, half = self.n, self.n // 2
        fwd = [(i, (i + 1) % n) for i in range(n)]
        bwd = [(i, (i - 1) % n) for i in range(n)]
        self.hop += 1
        if self.hop < half:
            self.left = lax.ppermute(self.left, self.axis, fwd)
            self.right = lax.ppermute(self.right, self.axis, bwd)
        else:
            m = self.piece.shape[0] // 2
            self.left = lax.ppermute(self.left[:m], self.axis, fwd)
            self.right = lax.ppermute(self.right[m:], self.axis, bwd)

    def record(self):
        if self.hop < self.n // 2:
            self.got += [(-self.hop, self.left), (self.hop, self.right)]
        else:
            self.got.append((self.hop, jnp.concatenate([self.left, self.right], axis=0)))

    def result(self):
        by_offset = dict([(0, self.piece)] + [(off % self.n, val) for off, val in self.got])
        ordered = jnp.stack([by_offset[k] for k in range(self.n)], axis=self.along)
        idx = lax.axis_index(self.axis)
        return jnp.take(ordered, (jnp.arange(self.n) - idx) % self.n, axis=self.along)


def lockstep(rings):
    live = [r for r in rings if r.active()]
    for r in live:
        r.step()
    held = lax.optimization_barrier(tuple((r.left, r.right) for r in live))
    for r, (left, right) in zip(live, held):
        r.left, r.right = left, right
        r.record()


def ring_reduce_scatter(chunks, axis, n):
    idx = lax.axis_index(axis)
    fwd = [(i, (i + 1) % n) for i in range(n)]
    bwd = [(i, (i - 1) % n) for i in range(n)]
    pick = lambda at: lax.dynamic_index_in_dim(chunks, at % n, 0, keepdims=False).astype(jnp.float32)
    half = n // 2
    m = chunks.shape[1] // 2
    to_right = pick(idx + half)[:m]
    to_left = pick(idx - half)[m:]
    for k in range(2, half + 1):
        got_left = lax.ppermute(to_right.astype(chunks.dtype), axis, fwd).astype(jnp.float32)
        got_right = lax.ppermute(to_left.astype(chunks.dtype), axis, bwd).astype(jnp.float32)
        own_r = pick(idx + half - k + 1)
        own_l = pick(idx - half + k - 1)
        if k == 2:
            to_right = own_r.at[:m].add(got_left)
            to_left = own_l.at[m:].add(got_right)
        else:
            to_right = own_r + got_left
            to_left = own_l + got_right
    got_left = lax.ppermute(to_right.astype(chunks.dtype), axis, fwd).astype(jnp.float32)
    got_right = lax.ppermute(to_left.astype(chunks.dtype), axis, bwd).astype(jnp.float32)
    return pick(idx) + got_left + got_right


def on_device(tokens, cotangent, route_weights, expert_ids, w_gate, w_up, w_down):
    tok_count, model_width = tokens.shape
    top_count = expert_ids.shape[1]
    experts = lax.axis_size("expert")
    shares = lax.axis_size("etp")
    part = model_width // shares
    share_idx = lax.axis_index("etp")
    capacity = tok_count // experts * top_count + min(top_count, tok_count % experts)
    slot_rows = experts * capacity
    named_count = jnp.sum(
        (expert_ids[:, :, None] == jnp.arange(experts, dtype=jnp.int32)).astype(jnp.int32), axis=1
    )
    before = jnp.cumsum(named_count, axis=0) - named_count
    position = jnp.take_along_axis(before, expert_ids, axis=1)
    slot_index = (expert_ids * capacity + position).reshape(-1)

    tok_part = lax.dynamic_slice_in_dim(tokens, share_idx * part, part, axis=1)
    cot_part = lax.dynamic_slice_in_dim(cotangent, share_idx * part, part, axis=1)
    copies = jnp.broadcast_to(tok_part[:, None, :], (tok_count, top_count, part))
    scaled = (route_weights[:, :, None] * cot_part[:, None, :].astype(jnp.float32)).astype(jnp.bfloat16)
    both = jnp.concatenate([copies, scaled], axis=2).reshape(-1, 2 * part)
    empty_slots = jnp.zeros((slot_rows, 2 * part), jnp.bfloat16)
    send = empty_slots.at[slot_index].set(both).reshape(experts, capacity, 2 * part)
    recv = lax.all_to_all(send, "expert", split_axis=0, concat_axis=0, tiled=True)

    gate_full = lax.all_gather(w_gate[0], "dp", axis=1, tiled=True)
    up_full = lax.all_gather(w_up[0], "dp", axis=1, tiled=True)
    downs = Ring(w_down[0], "dp", lax.axis_size("dp"), along=1)
    lockstep([downs])
    downs.left, downs.right, recv = lax.optimization_barrier((downs.left, downs.right, recv))
    rows = Ring(recv.reshape(slot_rows, 2 * part), "etp", shares)
    while downs.active() or rows.active():
        lockstep([downs, rows])
    down_full = downs.result().reshape(w_down.shape[1], model_width)
    gathered = rows.result()
    rows4 = gathered[:, :, :part]
    grads4 = gathered[:, :, part:]

    hidden_units = gate_full.shape[0]
    gate4 = gate_full.reshape(hidden_units, shares, part)
    up4 = up_full.reshape(hidden_units, shares, part)
    down4 = down_full.reshape(hidden_units, shares, part)

    gate_value = jnp.einsum("jsc,fjc->sf", rows4, gate4, preferred_element_type=jnp.float32)
    up_value = jnp.einsum("jsc,fjc->sf", rows4, up4, preferred_element_type=jnp.float32)
    sigmoid_gate = jax.nn.sigmoid(gate_value)
    active = gate_value * sigmoid_gate
    hidden = (active * up_value).astype(jnp.bfloat16)
    mixed4 = jnp.einsum("sf,fjc->jsc", hidden, down4, preferred_element_type=jnp.float32).astype(
        jnp.bfloat16
    )
    d_hidden = jnp.einsum("jsc,fjc->sf", grads4, down4, preferred_element_type=jnp.float32)
    d_gate = (
        d_hidden * up_value * sigmoid_gate * (1.0 + gate_value * (1.0 - sigmoid_gate))
    ).astype(jnp.bfloat16)
    d_up = (d_hidden * active).astype(jnp.bfloat16)
    input4 = (
        jnp.einsum("sf,fjc->jsc", d_gate, gate4, preferred_element_type=jnp.float32)
        + jnp.einsum("sf,fjc->jsc", d_up, up4, preferred_element_type=jnp.float32)
    ).astype(jnp.bfloat16)
    gate_term = jnp.einsum(
        "sf,jsc->fjc", d_gate, rows4, preferred_element_type=jnp.float32
    ).astype(jnp.bfloat16).reshape(hidden_units, model_width)
    weight_grads = lax.psum_scatter(gate_term, "dp", scatter_dimension=1, tiled=True)
    grad_gate = weight_grads.astype(jnp.float32)[None]

    outs4 = jnp.concatenate([mixed4, input4], axis=2)
    slot_out = ring_reduce_scatter(outs4, "etp", shares).astype(jnp.bfloat16)
    back = lax.all_to_all(
        slot_out.reshape(experts, capacity, 2 * part), "expert", split_axis=0, concat_axis=0, tiled=True
    )
    token_out = back.reshape(slot_rows, 2 * part)[slot_index].reshape(tok_count, top_count, 2 * part)
    token_out = token_out.astype(jnp.float32)
    mixed = jnp.sum(route_weights[:, :, None] * token_out[:, :, :part], axis=1)
    grad_tokens = jnp.sum(token_out[:, :, part:], axis=1)
    return (mixed.astype(jnp.bfloat16), grad_tokens.astype(jnp.bfloat16), grad_gate)


def solution(mesh):
    in_specs = (
        P(("dp", "expert"), None),
        P(("dp", "expert"), None),
        P(("dp", "expert"), None),
        P(("dp", "expert"), None),
        P("expert", "etp", "dp"),
        P("expert", "etp", "dp"),
        P("expert", "etp", "dp"),
    )
    out_specs = (P(("dp", "expert"), "etp"), P(("dp", "expert"), "etp"), P("expert", "etp", "dp"))
    return jax.shard_map(
        on_device, mesh=mesh, in_specs=in_specs, out_specs=out_specs, check_vma=False
    )
```

```python
import jax
import jax.numpy as jnp
from jax import lax
from jax.sharding import PartitionSpec as P


def ring_gather(piece, axis, n, along=0, tie=None):
    idx = lax.axis_index(axis)
    fwd = [(i, (i + 1) % n) for i in range(n)]
    bwd = [(i, (i - 1) % n) for i in range(n)]
    shape = list(piece.shape)
    shape.insert(along, n)
    out = jnp.zeros(shape, piece.dtype)
    put = lambda buf, val, at: lax.dynamic_update_index_in_dim(buf, val, at % n, along)
    out = put(out, piece, idx)
    left = right = piece
    half = n // 2
    for k in range(1, half):
        left = lax.ppermute(left, axis, fwd)
        right = lax.ppermute(right, axis, bwd)
        if k == 1 and tie is not None:
            left, right, tie = lax.optimization_barrier((left, right, tie))
        out = put(out, left, idx - k)
        out = put(out, right, idx + k)
    m = piece.shape[0] // 2
    first = lax.ppermute(left[:m], axis, fwd)
    second = lax.ppermute(right[m:], axis, bwd)
    out = put(out, jnp.concatenate([first, second], axis=0), idx + half)
    return out if tie is None else (out, tie)


def ring_reduce_scatter(chunks, axis, n):
    idx = lax.axis_index(axis)
    fwd = [(i, (i + 1) % n) for i in range(n)]
    bwd = [(i, (i - 1) % n) for i in range(n)]
    pick = lambda at: lax.dynamic_index_in_dim(chunks, at % n, 0, keepdims=False).astype(jnp.float32)
    half = n // 2
    m = chunks.shape[1] // 2
    to_right = pick(idx + half)[:m]
    to_left = pick(idx - half)[m:]
    for k in range(2, half + 1):
        got_left = lax.ppermute(to_right.astype(chunks.dtype), axis, fwd).astype(jnp.float32)
        got_right = lax.ppermute(to_left.astype(chunks.dtype), axis, bwd).astype(jnp.float32)
        own_r = pick(idx + half - k + 1)
        own_l = pick(idx - half + k - 1)
        if k == 2:
            to_right = own_r.at[:m].add(got_left)
            to_left = own_l.at[m:].add(got_right)
        else:
            to_right = own_r + got_left
            to_left = own_l + got_right
    got_left = lax.ppermute(to_right.astype(chunks.dtype), axis, fwd).astype(jnp.float32)
    got_right = lax.ppermute(to_left.astype(chunks.dtype), axis, bwd).astype(jnp.float32)
    return pick(idx) + got_left + got_right


def on_device(tokens, cotangent, route_weights, expert_ids, w_gate, w_up, w_down):
    tok_count, model_width = tokens.shape
    top_count = expert_ids.shape[1]
    experts = lax.axis_size("expert")
    shares = lax.axis_size("etp")
    part = model_width // shares
    share_idx = lax.axis_index("etp")
    capacity = tok_count // experts * top_count + min(top_count, tok_count % experts)
    slot_rows = experts * capacity
    named_count = jnp.sum(
        (expert_ids[:, :, None] == jnp.arange(experts, dtype=jnp.int32)).astype(jnp.int32), axis=1
    )
    before = jnp.cumsum(named_count, axis=0) - named_count
    position = jnp.take_along_axis(before, expert_ids, axis=1)
    slot_index = (expert_ids * capacity + position).reshape(-1)

    tok_part = lax.dynamic_slice_in_dim(tokens, share_idx * part, part, axis=1)
    cot_part = lax.dynamic_slice_in_dim(cotangent, share_idx * part, part, axis=1)
    copies = jnp.broadcast_to(tok_part[:, None, :], (tok_count, top_count, part))
    scaled = (route_weights[:, :, None] * cot_part[:, None, :].astype(jnp.float32)).astype(jnp.bfloat16)
    both = jnp.concatenate([copies, scaled], axis=2).reshape(-1, 2 * part)
    empty_slots = jnp.zeros((slot_rows, 2 * part), jnp.bfloat16)
    send = empty_slots.at[slot_index].set(both).reshape(experts, capacity, 2 * part)
    recv = lax.all_to_all(send, "expert", split_axis=0, concat_axis=0, tiled=True)
    down_ring, recv = ring_gather(w_down[0], "dp", lax.axis_size("dp"), along=1, tie=recv)
    down_full = down_ring.reshape(w_down.shape[1], -1)
    gathered = ring_gather(recv.reshape(slot_rows, 2 * part), "etp", shares)
    rows4 = gathered[:, :, :part]
    grads4 = gathered[:, :, part:]

    gate_full = lax.all_gather(w_gate[0], "dp", axis=1, tiled=True)
    up_full = lax.all_gather(w_up[0], "dp", axis=1, tiled=True)
    hidden_units = gate_full.shape[0]
    gate4 = gate_full.reshape(hidden_units, shares, part)
    up4 = up_full.reshape(hidden_units, shares, part)
    down4 = down_full.reshape(hidden_units, shares, part)

    gate_value = jnp.einsum("jsc,fjc->sf", rows4, gate4, preferred_element_type=jnp.float32)
    up_value = jnp.einsum("jsc,fjc->sf", rows4, up4, preferred_element_type=jnp.float32)
    sigmoid_gate = jax.nn.sigmoid(gate_value)
    active = gate_value * sigmoid_gate
    hidden = (active * up_value).astype(jnp.bfloat16)
    mixed4 = jnp.einsum("sf,fjc->jsc", hidden, down4, preferred_element_type=jnp.float32).astype(
        jnp.bfloat16
    )
    d_hidden = jnp.einsum("jsc,fjc->sf", grads4, down4, preferred_element_type=jnp.float32)
    d_gate = (
        d_hidden * up_value * sigmoid_gate * (1.0 + gate_value * (1.0 - sigmoid_gate))
    ).astype(jnp.bfloat16)
    d_up = (d_hidden * active).astype(jnp.bfloat16)
    input4 = (
        jnp.einsum("sf,fjc->jsc", d_gate, gate4, preferred_element_type=jnp.float32)
        + jnp.einsum("sf,fjc->jsc", d_up, up4, preferred_element_type=jnp.float32)
    ).astype(jnp.bfloat16)
    gate_term = jnp.einsum(
        "sf,jsc->fjc", d_gate, rows4, preferred_element_type=jnp.float32
    ).astype(jnp.bfloat16).reshape(hidden_units, model_width)
    weight_grads = lax.psum_scatter(gate_term, "dp", scatter_dimension=1, tiled=True)
    grad_gate = weight_grads.astype(jnp.float32)[None]

    outs4 = jnp.concatenate([mixed4, input4], axis=2)
    slot_out = ring_reduce_scatter(outs4, "etp", shares).astype(jnp.bfloat16)
    back = lax.all_to_all(
        slot_out.reshape(experts, capacity, 2 * part), "expert", split_axis=0, concat_axis=0, tiled=True
    )
    token_out = back.reshape(slot_rows, 2 * part)[slot_index].reshape(tok_count, top_count, 2 * part)
    token_out = token_out.astype(jnp.float32)
    mixed = jnp.sum(route_weights[:, :, None] * token_out[:, :, :part], axis=1)
    grad_tokens = jnp.sum(token_out[:, :, part:], axis=1)
    return (mixed.astype(jnp.bfloat16), grad_tokens.astype(jnp.bfloat16), grad_gate)


def solution(mesh):
    in_specs = (
        P(("dp", "expert"), None),
        P(("dp", "expert"), None),
        P(("dp", "expert"), None),
        P(("dp", "expert"), None),
        P("expert", "etp", "dp"),
        P("expert", "etp", "dp"),
        P("expert", "etp", "dp"),
    )
    out_specs = (P(("dp", "expert"), "etp"), P(("dp", "expert"), "etp"), P("expert", "etp", "dp"))
    return jax.shard_map(
        on_device, mesh=mesh, in_specs=in_specs, out_specs=out_specs, check_vma=False
    )
```

```python
import jax
import jax.numpy as jnp
from jax import lax
from jax.sharding import PartitionSpec as P


class Ring:
    def __init__(self, piece, axis, n, along=0):
        self.piece, self.axis, self.n, self.along = piece, axis, n, along
        self.left = self.right = piece
        self.hop = 0
        self.got = []

    def active(self):
        return self.hop < self.n // 2

    def step(self):
        n, half = self.n, self.n // 2
        fwd = [(i, (i + 1) % n) for i in range(n)]
        bwd = [(i, (i - 1) % n) for i in range(n)]
        self.hop += 1
        if self.hop < half:
            self.left = lax.ppermute(self.left, self.axis, fwd)
            self.right = lax.ppermute(self.right, self.axis, bwd)
        else:
            m = self.piece.shape[0] // 2
            self.left = lax.ppermute(self.left[:m], self.axis, fwd)
            self.right = lax.ppermute(self.right[m:], self.axis, bwd)

    def record(self):
        if self.hop < self.n // 2:
            self.got += [(-self.hop, self.left), (self.hop, self.right)]
        else:
            self.got.append((self.hop, jnp.concatenate([self.left, self.right], axis=0)))

    def result(self):
        idx = lax.axis_index(self.axis)
        shape = list(self.piece.shape)
        shape.insert(self.along, self.n)
        out = jnp.zeros(shape, self.piece.dtype)
        for offset, val in [(0, self.piece)] + self.got:
            out = lax.dynamic_update_index_in_dim(out, val, (idx + offset) % self.n, self.along)
        return out


def lockstep(rings):
    live = [r for r in rings if r.active()]
    for r in live:
        r.step()
    held = lax.optimization_barrier(tuple((r.left, r.right) for r in live))
    for r, (left, right) in zip(live, held):
        r.left, r.right = left, right
        r.record()


def ring_reduce_scatter(chunks, axis, n):
    idx = lax.axis_index(axis)
    fwd = [(i, (i + 1) % n) for i in range(n)]
    bwd = [(i, (i - 1) % n) for i in range(n)]
    pick = lambda at: lax.dynamic_index_in_dim(chunks, at % n, 0, keepdims=False).astype(jnp.float32)
    half = n // 2
    m = chunks.shape[1] // 2
    to_right = pick(idx + half)[:m]
    to_left = pick(idx - half)[m:]
    for k in range(2, half + 1):
        got_left = lax.ppermute(to_right.astype(chunks.dtype), axis, fwd).astype(jnp.float32)
        got_right = lax.ppermute(to_left.astype(chunks.dtype), axis, bwd).astype(jnp.float32)
        own_r = pick(idx + half - k + 1)
        own_l = pick(idx - half + k - 1)
        if k == 2:
            to_right = own_r.at[:m].add(got_left)
            to_left = own_l.at[m:].add(got_right)
        else:
            to_right = own_r + got_left
            to_left = own_l + got_right
    got_left = lax.ppermute(to_right.astype(chunks.dtype), axis, fwd).astype(jnp.float32)
    got_right = lax.ppermute(to_left.astype(chunks.dtype), axis, bwd).astype(jnp.float32)
    return pick(idx) + got_left + got_right


def on_device(tokens, cotangent, route_weights, expert_ids, w_gate, w_up, w_down):
    tok_count, model_width = tokens.shape
    top_count = expert_ids.shape[1]
    experts = lax.axis_size("expert")
    shares = lax.axis_size("etp")
    part = model_width // shares
    share_idx = lax.axis_index("etp")
    capacity = tok_count // experts * top_count + min(top_count, tok_count % experts)
    slot_rows = experts * capacity
    named_count = jnp.sum(
        (expert_ids[:, :, None] == jnp.arange(experts, dtype=jnp.int32)).astype(jnp.int32), axis=1
    )
    before = jnp.cumsum(named_count, axis=0) - named_count
    position = jnp.take_along_axis(before, expert_ids, axis=1)
    slot_index = (expert_ids * capacity + position).reshape(-1)

    tok_part = lax.dynamic_slice_in_dim(tokens, share_idx * part, part, axis=1)
    cot_part = lax.dynamic_slice_in_dim(cotangent, share_idx * part, part, axis=1)
    copies = jnp.broadcast_to(tok_part[:, None, :], (tok_count, top_count, part))
    scaled = (route_weights[:, :, None] * cot_part[:, None, :].astype(jnp.float32)).astype(jnp.bfloat16)
    both = jnp.concatenate([copies, scaled], axis=2).reshape(-1, 2 * part)
    empty_slots = jnp.zeros((slot_rows, 2 * part), jnp.bfloat16)
    send = empty_slots.at[slot_index].set(both).reshape(experts, capacity, 2 * part)
    recv = lax.all_to_all(send, "expert", split_axis=0, concat_axis=0, tiled=True)

    downs = Ring(w_down[0], "dp", lax.axis_size("dp"), along=1)
    lockstep([downs])
    downs.left, downs.right, recv = lax.optimization_barrier((downs.left, downs.right, recv))
    rows = Ring(recv.reshape(slot_rows, 2 * part), "etp", shares)
    lockstep([downs, rows])
    for ring in (downs, rows, downs):
        ring.step()
        ring.record()
    down_full = downs.result().reshape(w_down.shape[1], model_width)
    gathered = rows.result()
    rows4 = gathered[:, :, :part]
    grads4 = gathered[:, :, part:]

    gate_full = lax.all_gather(w_gate[0], "dp", axis=1, tiled=True)
    up_full = lax.all_gather(w_up[0], "dp", axis=1, tiled=True)
    hidden_units = gate_full.shape[0]
    gate4 = gate_full.reshape(hidden_units, shares, part)
    up4 = up_full.reshape(hidden_units, shares, part)
    down4 = down_full.reshape(hidden_units, shares, part)

    gate_value = jnp.einsum("jsc,fjc->sf", rows4, gate4, preferred_element_type=jnp.float32)
    up_value = jnp.einsum("jsc,fjc->sf", rows4, up4, preferred_element_type=jnp.float32)
    sigmoid_gate = jax.nn.sigmoid(gate_value)
    active = gate_value * sigmoid_gate
    hidden = (active * up_value).astype(jnp.bfloat16)
    mixed4 = jnp.einsum("sf,fjc->jsc", hidden, down4, preferred_element_type=jnp.float32).astype(
        jnp.bfloat16
    )
    d_hidden = jnp.einsum("jsc,fjc->sf", grads4, down4, preferred_element_type=jnp.float32)
    d_gate = (
        d_hidden * up_value * sigmoid_gate * (1.0 + gate_value * (1.0 - sigmoid_gate))
    ).astype(jnp.bfloat16)
    d_up = (d_hidden * active).astype(jnp.bfloat16)
    input4 = (
        jnp.einsum("sf,fjc->jsc", d_gate, gate4, preferred_element_type=jnp.float32)
        + jnp.einsum("sf,fjc->jsc", d_up, up4, preferred_element_type=jnp.float32)
    ).astype(jnp.bfloat16)
    gate_term = jnp.einsum(
        "sf,jsc->fjc", d_gate, rows4, preferred_element_type=jnp.float32
    ).astype(jnp.bfloat16).reshape(hidden_units, model_width)
    weight_grads = lax.psum_scatter(gate_term, "dp", scatter_dimension=1, tiled=True)
    grad_gate = weight_grads.astype(jnp.float32)[None]

    outs4 = jnp.concatenate([mixed4, input4], axis=2)
    slot_out = ring_reduce_scatter(outs4, "etp", shares).astype(jnp.bfloat16)
    back = lax.all_to_all(
        slot_out.reshape(experts, capacity, 2 * part), "expert", split_axis=0, concat_axis=0, tiled=True
    )
    token_out = back.reshape(slot_rows, 2 * part)[slot_index].reshape(tok_count, top_count, 2 * part)
    token_out = token_out.astype(jnp.float32)
    mixed = jnp.sum(route_weights[:, :, None] * token_out[:, :, :part], axis=1)
    grad_tokens = jnp.sum(token_out[:, :, part:], axis=1)
    return (mixed.astype(jnp.bfloat16), grad_tokens.astype(jnp.bfloat16), grad_gate)


def solution(mesh):
    in_specs = (
        P(("dp", "expert"), None),
        P(("dp", "expert"), None),
        P(("dp", "expert"), None),
        P(("dp", "expert"), None),
        P("expert", "etp", "dp"),
        P("expert", "etp", "dp"),
        P("expert", "etp", "dp"),
    )
    out_specs = (P(("dp", "expert"), "etp"), P(("dp", "expert"), "etp"), P("expert", "etp", "dp"))
    return jax.shard_map(
        on_device, mesh=mesh, in_specs=in_specs, out_specs=out_specs, check_vma=False
    )
```

```python
import jax
import jax.numpy as jnp
from jax import lax
from jax.sharding import PartitionSpec as P


class Ring:
    def __init__(self, piece, axis, n, along=0):
        self.piece, self.axis, self.n, self.along = piece, axis, n, along
        self.left = self.right = piece
        self.hop = 0
        self.got = []

    def active(self):
        return self.hop < self.n // 2

    def step(self):
        n, half = self.n, self.n // 2
        fwd = [(i, (i + 1) % n) for i in range(n)]
        bwd = [(i, (i - 1) % n) for i in range(n)]
        self.hop += 1
        if self.hop < half:
            self.left = lax.ppermute(self.left, self.axis, fwd)
            self.right = lax.ppermute(self.right, self.axis, bwd)
        else:
            m = self.piece.shape[0] // 2
            self.left = lax.ppermute(self.left[:m], self.axis, fwd)
            self.right = lax.ppermute(self.right[m:], self.axis, bwd)

    def record(self):
        if self.hop < self.n // 2:
            self.got += [(-self.hop, self.left), (self.hop, self.right)]
        else:
            self.got.append((self.hop, jnp.concatenate([self.left, self.right], axis=0)))

    def result(self):
        idx = lax.axis_index(self.axis)
        shape = list(self.piece.shape)
        shape.insert(self.along, self.n)
        out = jnp.zeros(shape, self.piece.dtype)
        for offset, val in [(0, self.piece)] + self.got:
            out = lax.dynamic_update_index_in_dim(out, val, (idx + offset) % self.n, self.along)
        return out


def lockstep(rings):
    live = [r for r in rings if r.active()]
    for r in live:
        r.step()
    held = lax.optimization_barrier(tuple((r.left, r.right) for r in live))
    for r, (left, right) in zip(live, held):
        r.left, r.right = left, right
        r.record()


def ring_reduce_scatter(chunks, axis, n):
    idx = lax.axis_index(axis)
    fwd = [(i, (i + 1) % n) for i in range(n)]
    bwd = [(i, (i - 1) % n) for i in range(n)]
    pick = lambda at: lax.dynamic_index_in_dim(chunks, at % n, 0, keepdims=False).astype(jnp.float32)
    half = n // 2
    m = chunks.shape[1] // 2
    to_right = pick(idx + half)[:m]
    to_left = pick(idx - half)[m:]
    for k in range(2, half + 1):
        got_left = lax.ppermute(to_right.astype(chunks.dtype), axis, fwd).astype(jnp.float32)
        got_right = lax.ppermute(to_left.astype(chunks.dtype), axis, bwd).astype(jnp.float32)
        own_r = pick(idx + half - k + 1)
        own_l = pick(idx - half + k - 1)
        if k == 2:
            to_right = own_r.at[:m].add(got_left)
            to_left = own_l.at[m:].add(got_right)
        else:
            to_right = own_r + got_left
            to_left = own_l + got_right
    got_left = lax.ppermute(to_right.astype(chunks.dtype), axis, fwd).astype(jnp.float32)
    got_right = lax.ppermute(to_left.astype(chunks.dtype), axis, bwd).astype(jnp.float32)
    return pick(idx) + got_left + got_right


def on_device(tokens, cotangent, route_weights, expert_ids, w_gate, w_up, w_down):
    tok_count, model_width = tokens.shape
    top_count = expert_ids.shape[1]
    experts = lax.axis_size("expert")
    shares = lax.axis_size("etp")
    part = model_width // shares
    share_idx = lax.axis_index("etp")
    capacity = tok_count // experts * top_count + min(top_count, tok_count % experts)
    slot_rows = experts * capacity
    named_count = jnp.sum(
        (expert_ids[:, :, None] == jnp.arange(experts, dtype=jnp.int32)).astype(jnp.int32), axis=1
    )
    before = jnp.cumsum(named_count, axis=0) - named_count
    position = jnp.take_along_axis(before, expert_ids, axis=1)
    slot_index = (expert_ids * capacity + position).reshape(-1)

    tok_part = lax.dynamic_slice_in_dim(tokens, share_idx * part, part, axis=1)
    cot_part = lax.dynamic_slice_in_dim(cotangent, share_idx * part, part, axis=1)
    copies = jnp.broadcast_to(tok_part[:, None, :], (tok_count, top_count, part))
    scaled = (route_weights[:, :, None] * cot_part[:, None, :].astype(jnp.float32)).astype(jnp.bfloat16)
    both = jnp.concatenate([copies, scaled], axis=2).reshape(-1, 2 * part)
    empty_slots = jnp.zeros((slot_rows, 2 * part), jnp.bfloat16)
    send = empty_slots.at[slot_index].set(both).reshape(experts, capacity, 2 * part)
    recv = lax.all_to_all(send, "expert", split_axis=0, concat_axis=0, tiled=True)

    downs = Ring(w_down[0], "dp", lax.axis_size("dp"), along=1)
    lockstep([downs])
    downs.left, downs.right, recv = lax.optimization_barrier((downs.left, downs.right, recv))
    rows = Ring(recv.reshape(slot_rows, 2 * part), "etp", shares)
    lockstep([downs, rows])
    for ring in (downs, rows, downs):
        ring.step()
        ring.record()
    down_full = downs.result().reshape(w_down.shape[1], model_width)
    gathered = rows.result()
    rows4 = gathered[:, :, :part]
    grads4 = gathered[:, :, part:]

    gate_full, up_full = lax.all_gather(jnp.stack([w_gate[0], w_up[0]]), "dp", axis=2, tiled=True)
    hidden_units = gate_full.shape[0]
    gate4 = gate_full.reshape(hidden_units, shares, part)
    up4 = up_full.reshape(hidden_units, shares, part)
    down4 = down_full.reshape(hidden_units, shares, part)

    gate_value = jnp.einsum("jsc,fjc->sf", rows4, gate4, preferred_element_type=jnp.float32)
    up_value = jnp.einsum("jsc,fjc->sf", rows4, up4, preferred_element_type=jnp.float32)
    sigmoid_gate = jax.nn.sigmoid(gate_value)
    active = gate_value * sigmoid_gate
    hidden = (active * up_value).astype(jnp.bfloat16)
    mixed4 = jnp.einsum("sf,fjc->jsc", hidden, down4, preferred_element_type=jnp.float32).astype(
        jnp.bfloat16
    )
    d_hidden = jnp.einsum("jsc,fjc->sf", grads4, down4, preferred_element_type=jnp.float32)
    d_gate = (
        d_hidden * up_value * sigmoid_gate * (1.0 + gate_value * (1.0 - sigmoid_gate))
    ).astype(jnp.bfloat16)
    d_up = (d_hidden * active).astype(jnp.bfloat16)
    input4 = (
        jnp.einsum("sf,fjc->jsc", d_gate, gate4, preferred_element_type=jnp.float32)
        + jnp.einsum("sf,fjc->jsc", d_up, up4, preferred_element_type=jnp.float32)
    ).astype(jnp.bfloat16)
    gate_term = jnp.einsum(
        "sf,jsc->fjc", d_gate, rows4, preferred_element_type=jnp.float32
    ).astype(jnp.bfloat16).reshape(hidden_units, model_width)
    weight_grads = lax.psum_scatter(gate_term, "dp", scatter_dimension=1, tiled=True)
    grad_gate = weight_grads.astype(jnp.float32)[None]

    outs4 = jnp.concatenate([mixed4, input4], axis=2)
    slot_out = ring_reduce_scatter(outs4, "etp", shares).astype(jnp.bfloat16)
    back = lax.all_to_all(
        slot_out.reshape(experts, capacity, 2 * part), "expert", split_axis=0, concat_axis=0, tiled=True
    )
    token_out = back.reshape(slot_rows, 2 * part)[slot_index].reshape(tok_count, top_count, 2 * part)
    token_out = token_out.astype(jnp.float32)
    mixed = jnp.sum(route_weights[:, :, None] * token_out[:, :, :part], axis=1)
    grad_tokens = jnp.sum(token_out[:, :, part:], axis=1)
    return (mixed.astype(jnp.bfloat16), grad_tokens.astype(jnp.bfloat16), grad_gate)


def solution(mesh):
    in_specs = (
        P(("dp", "expert"), None),
        P(("dp", "expert"), None),
        P(("dp", "expert"), None),
        P(("dp", "expert"), None),
        P("expert", "etp", "dp"),
        P("expert", "etp", "dp"),
        P("expert", "etp", "dp"),
    )
    out_specs = (P(("dp", "expert"), "etp"), P(("dp", "expert"), "etp"), P("expert", "etp", "dp"))
    return jax.shard_map(
        on_device, mesh=mesh, in_specs=in_specs, out_specs=out_specs, check_vma=False
    )
```

```python
import jax
import jax.numpy as jnp
from jax import lax
from jax.sharding import PartitionSpec as P


class Ring:
    def __init__(self, piece, axis, n, along=0):
        self.piece, self.axis, self.n, self.along = piece, axis, n, along
        self.left = self.right = piece
        self.hop = 0
        self.got = []

    def active(self):
        return self.hop < self.n // 2

    def step(self):
        n, half = self.n, self.n // 2
        fwd = [(i, (i + 1) % n) for i in range(n)]
        bwd = [(i, (i - 1) % n) for i in range(n)]
        self.hop += 1
        if self.hop < half:
            self.left = lax.ppermute(self.left, self.axis, fwd)
            self.right = lax.ppermute(self.right, self.axis, bwd)
        else:
            m = self.piece.shape[0] // 2
            self.left = lax.ppermute(self.left[:m], self.axis, fwd)
            self.right = lax.ppermute(self.right[m:], self.axis, bwd)

    def record(self):
        if self.hop < self.n // 2:
            self.got += [(-self.hop, self.left), (self.hop, self.right)]
        else:
            self.got.append((self.hop, jnp.concatenate([self.left, self.right], axis=0)))

    def result(self):
        idx = lax.axis_index(self.axis)
        shape = list(self.piece.shape)
        shape.insert(self.along, self.n)
        out = jnp.zeros(shape, self.piece.dtype)
        for offset, val in [(0, self.piece)] + self.got:
            out = lax.dynamic_update_index_in_dim(out, val, (idx + offset) % self.n, self.along)
        return out


def lockstep(rings):
    live = [r for r in rings if r.active()]
    for r in live:
        r.step()
    held = lax.optimization_barrier(tuple((r.left, r.right) for r in live))
    for r, (left, right) in zip(live, held):
        r.left, r.right = left, right
        r.record()


def ring_reduce_scatter(chunks, axis, n):
    idx = lax.axis_index(axis)
    fwd = [(i, (i + 1) % n) for i in range(n)]
    bwd = [(i, (i - 1) % n) for i in range(n)]
    pick = lambda at: lax.dynamic_index_in_dim(chunks, at % n, 0, keepdims=False).astype(jnp.float32)
    half = n // 2
    m = chunks.shape[1] // 2
    to_right = pick(idx + half)[:m]
    to_left = pick(idx - half)[m:]
    for k in range(2, half + 1):
        got_left = lax.ppermute(to_right.astype(chunks.dtype), axis, fwd).astype(jnp.float32)
        got_right = lax.ppermute(to_left.astype(chunks.dtype), axis, bwd).astype(jnp.float32)
        own_r = pick(idx + half - k + 1)
        own_l = pick(idx - half + k - 1)
        if k == 2:
            to_right = own_r.at[:m].add(got_left)
            to_left = own_l.at[m:].add(got_right)
        else:
            to_right = own_r + got_left
            to_left = own_l + got_right
    got_left = lax.ppermute(to_right.astype(chunks.dtype), axis, fwd).astype(jnp.float32)
    got_right = lax.ppermute(to_left.astype(chunks.dtype), axis, bwd).astype(jnp.float32)
    return pick(idx) + got_left + got_right


def on_device(tokens, cotangent, route_weights, expert_ids, w_gate, w_up, w_down):
    tok_count, model_width = tokens.shape
    top_count = expert_ids.shape[1]
    experts = lax.axis_size("expert")
    shares = lax.axis_size("etp")
    part = model_width // shares
    share_idx = lax.axis_index("etp")
    capacity = tok_count // experts * top_count + min(top_count, tok_count % experts)
    slot_rows = experts * capacity
    named_count = jnp.sum(
        (expert_ids[:, :, None] == jnp.arange(experts, dtype=jnp.int32)).astype(jnp.int32), axis=1
    )
    before = jnp.cumsum(named_count, axis=0) - named_count
    position = jnp.take_along_axis(before, expert_ids, axis=1)
    slot_index = (expert_ids * capacity + position).reshape(-1)

    tok_part = lax.dynamic_slice_in_dim(tokens, share_idx * part, part, axis=1)
    cot_part = lax.dynamic_slice_in_dim(cotangent, share_idx * part, part, axis=1)
    routes = tok_count * top_count
    owner = jnp.full((slot_rows,), routes, jnp.int32).at[slot_index].set(jnp.arange(routes, dtype=jnp.int32))
    owner_tok = owner // top_count
    zero_row = jnp.zeros((1, part), tokens.dtype)
    tok_pad = jnp.concatenate([tok_part, zero_row], axis=0)
    cot_pad = jnp.concatenate([cot_part, zero_row], axis=0)
    weight_pad = jnp.concatenate([route_weights.reshape(-1), jnp.zeros((1,), route_weights.dtype)])
    scaled = (weight_pad[owner][:, None] * cot_pad[owner_tok].astype(jnp.float32)).astype(jnp.bfloat16)
    send = jnp.concatenate([tok_pad[owner_tok], scaled], axis=1).reshape(experts, capacity, 2 * part)
    recv = lax.all_to_all(send, "expert", split_axis=0, concat_axis=0, tiled=True)

    downs = Ring(w_down[0], "dp", lax.axis_size("dp"), along=1)
    lockstep([downs])
    downs.left, downs.right, recv = lax.optimization_barrier((downs.left, downs.right, recv))
    rows = Ring(recv.reshape(slot_rows, 2 * part), "etp", shares)
    lockstep([downs, rows])
    for ring in (downs, rows, downs):
        ring.step()
        ring.record()
    down_full = downs.result().reshape(w_down.shape[1], model_width)
    gathered = rows.result()
    rows4 = gathered[:, :, :part]
    grads4 = gathered[:, :, part:]

    gate_full, up_full = lax.all_gather(jnp.stack([w_gate[0], w_up[0]]), "dp", axis=2, tiled=True)
    hidden_units = gate_full.shape[0]
    gate4 = gate_full.reshape(hidden_units, shares, part)
    up4 = up_full.reshape(hidden_units, shares, part)
    down4 = down_full.reshape(hidden_units, shares, part)

    gate_value = jnp.einsum("jsc,fjc->sf", rows4, gate4, preferred_element_type=jnp.float32)
    up_value = jnp.einsum("jsc,fjc->sf", rows4, up4, preferred_element_type=jnp.float32)
    sigmoid_gate = jax.nn.sigmoid(gate_value)
    active = gate_value * sigmoid_gate
    hidden = (active * up_value).astype(jnp.bfloat16)
    mixed4 = jnp.einsum("sf,fjc->jsc", hidden, down4, preferred_element_type=jnp.float32).astype(
        jnp.bfloat16
    )
    d_hidden = jnp.einsum("jsc,fjc->sf", grads4, down4, preferred_element_type=jnp.float32)
    d_gate = (
        d_hidden * up_value * sigmoid_gate * (1.0 + gate_value * (1.0 - sigmoid_gate))
    ).astype(jnp.bfloat16)
    d_up = (d_hidden * active).astype(jnp.bfloat16)
    input4 = (
        jnp.einsum("sf,fjc->jsc", d_gate, gate4, preferred_element_type=jnp.float32)
        + jnp.einsum("sf,fjc->jsc", d_up, up4, preferred_element_type=jnp.float32)
    ).astype(jnp.bfloat16)
    gate_term = jnp.einsum(
        "sf,jsc->fjc", d_gate, rows4, preferred_element_type=jnp.float32
    ).astype(jnp.bfloat16).reshape(hidden_units, model_width)
    weight_grads = lax.psum_scatter(gate_term, "dp", scatter_dimension=1, tiled=True)
    grad_gate = weight_grads.astype(jnp.float32)[None]

    outs4 = jnp.concatenate([mixed4, input4], axis=2)
    slot_out = ring_reduce_scatter(outs4, "etp", shares).astype(jnp.bfloat16)
    back = lax.all_to_all(
        slot_out.reshape(experts, capacity, 2 * part), "expert", split_axis=0, concat_axis=0, tiled=True
    )
    token_out = back.reshape(slot_rows, 2 * part)[slot_index].reshape(tok_count, top_count, 2 * part)
    token_out = token_out.astype(jnp.float32)
    mixed = jnp.sum(route_weights[:, :, None] * token_out[:, :, :part], axis=1)
    grad_tokens = jnp.sum(token_out[:, :, part:], axis=1)
    return (mixed.astype(jnp.bfloat16), grad_tokens.astype(jnp.bfloat16), grad_gate)


def solution(mesh):
    in_specs = (
        P(("dp", "expert"), None),
        P(("dp", "expert"), None),
        P(("dp", "expert"), None),
        P(("dp", "expert"), None),
        P("expert", "etp", "dp"),
        P("expert", "etp", "dp"),
        P("expert", "etp", "dp"),
    )
    out_specs = (P(("dp", "expert"), "etp"), P(("dp", "expert"), "etp"), P("expert", "etp", "dp"))
    return jax.shard_map(
        on_device, mesh=mesh, in_specs=in_specs, out_specs=out_specs, check_vma=False
    )
```
